512 devices in a mesh: seq: 128 (over y, z, core), tp: 4 (over x).
Axes of the slice: x: 4, y: 4, z: 16, core: 2. Of those that a mesh axis runs over, the one named last changes fastest.
Arguments:
- tokens: bfloat16 [32768, 1280], P('seq'), may hold values from -45 to 45
- ln_gain: float32 [1280], replicated, may hold values from 0.6 to 10, as said below
- ln_bias: float32 [1280], replicated, may hold values from -3 to 3
- w_qkv: bfloat16 [3, 1280, 1280], P(None, None, 'tp'), may hold values from -0.15625 to 0.15625
- b_qkv: float32 [3, 1280], P(None, 'tp'), may hold values from -3 to 3
- w_out: bfloat16 [1280, 1280], P('tp'), may hold values from -0.15625 to 0.15625
- b_out: float32 [1280], replicated, may hold values from -3 to 3
- merge_gain: float32 [1280], replicated, may hold values from 0.25 to 1.75
- merge_bias: float32 [1280], replicated, may hold values from -3 to 3
- segments: int32 [8192], replicated, may hold values from 0 to 63, never falling along the last dimension, each value on 1 to 256 neighbouring positions
- owners: int32 [8192, 1], P('seq'), may hold values from 0 to 127; in each aligned block of 64 rows (0 to 63, 64 to 127, ...) at most 2 rows name the same one
Outputs:
- routed: bfloat16 [32768, 5120], P('seq', 'tp')
The draws below stay inside these ranges and needn't reach their ends.
Inputs may be any that keep to these rules, and one draw needn't show every extreme that they name: `segments`: Non-decreasing along the rows; one image holds at most 256 merged rows, and some image holds exactly that many. `owners`: among the 64 merged rows of one device no owner is named more than 2 times, a bound that some block reaches. `ln_gain`: gains are positive, within 0.6 to 10.
All inputs are finite; a program needn't handle non-finite values.
Results may differ from the reference program's by a relative error of at most 0.024.
The reference program's roundings to bfloat16 on the way count: a program that leaves them out, or rounds other values in their place, can miss the bound.
Values may be sent and summed in bfloat16 or wider, within the bound.
No kernel may reach another device: no remote copies, remote signals or barrier semaphores. Data moves between devices by JAX's collectives and lax.ppermute only.
A program may use at most 64 MiB of HBM per device.

```python
import math
import jax
import jax.numpy as jnp
import numpy as np
from jax import lax

D = 1280
HEADS = 16
HEAD_DIM = 80
TOK_DEV = 256
SPAN = 4
TOKENS = 32768
GROUPS = 8192
MER_DEV = 64
IMAGES = 64
CAP = 2
N_SEQ = 128
N_TP = 4


def draw_tokens(key, part):
    key_rows, key_cols, key_vals = jax.random.split(key, 3)
    row_scale = jnp.exp(jax.random.uniform(key_rows, (TOKENS, 1), jnp.float32, -1.2, 1.2))
    col_scale = jnp.exp(jax.random.uniform(key_cols, (1, D), jnp.float32, -1.2, 1.2))
    base = jnp.clip(jax.random.normal(key_vals, (TOKENS, D), jnp.float32), -4.0, 4.0)
    return (base * row_scale * col_scale).astype(jnp.bfloat16)


def draw_ln_gain(key, part):
    return jnp.exp(jax.random.uniform(key, (D,), jnp.float32, -0.5, 0.5))


def block_scale(own_key, extent, cuts, least, largest):
    gain, own = 1.0, jax.random.fold_in(own_key, 6)
    for axis_at, parts in cuts:
        draws = jnp.exp(jax.random.uniform(jax.random.fold_in(own, axis_at), (parts,), jnp.float32, least / len(cuts), largest / len(cuts)))
        gain = gain * jnp.repeat(draws, extent[axis_at] // parts).reshape([-1 if axis == axis_at else 1 for axis in range(len(extent))])
    return gain


def length_profile(count, total, reach, skew):
    loads = [(1 << 20) // math.isqrt(rank ** skew) + 1 for rank in range(2, count + 1)]
    surplus, holding = total - reach - (count - 1), [1] * (count - 1)
    while surplus > 0:
        movable = [i for i in range(count - 1) if holding[i] < reach]
        whole, budget = sum([loads[i] for i in movable]), surplus
        for i in movable:
            more = min(reach - holding[i], max(1, budget * loads[i] // whole), surplus)
            holding[i] = holding[i] + more
            surplus = surplus - more
    return np.array([reach] + holding)


def ragged(own_key, number_of, total, limit, lean):
    if number_of == 2:
        one = jax.random.randint(own_key, (), max(1, total - limit), min(limit, total - 1) + 1)
        return jnp.stack([one, total - one])
    sizes = jnp.asarray(length_profile(number_of, total, limit, lean), jnp.int32)
    twos = (number_of - 1) // 2
    donor, taker = sizes[1:1 + 2 * twos:2], sizes[2:2 + 2 * twos:2]
    margin = jnp.minimum(donor - 1, limit - taker)
    passed = jax.random.randint(jax.random.fold_in(own_key, 1), (twos,), 0, 1 << 20) % (margin + 1)
    sizes = sizes.at[1:1 + 2 * twos:2].set(donor - passed).at[2:2 + 2 * twos:2].set(taker + passed)
    return sizes[jax.random.permutation(jax.random.fold_in(own_key, 2), number_of)]


def assign_block(key, own, number, rows, number_of, top, bound, slope):
    order = jax.random.permutation(key, number_of)
    heavy_load, usual = portions_of(number_of, rows * top, bound, slope, True), portions_of(number_of, rows * top, bound, slope, False)
    places = jnp.arange(number_of)

    def named(lengths, turn):
        used = int((lengths > 0).sum())
        fixed = max(1, used // 4)
        passed = fixed + (places - fixed + turn * (used - fixed)) % max(1, number_of - fixed)
        return jnp.zeros((number_of,), jnp.int32).at[order[jnp.where(places < fixed, places, passed)]].set(jnp.asarray(lengths, jnp.int32))

    lengths = jnp.where(number % 4 == 0, named(heavy_load, number // 4), named(usual, number - number // 4 - 1))
    mixed = jax.random.permutation(jax.random.fold_in(own, 3), number_of)
    donor, sink = mixed[0:number_of // 2 * 2:2], mixed[1:number_of // 2 * 2:2]
    margin = jnp.minimum(lengths[donor] - 1, bound - lengths[sink]) // 2
    margin = jnp.where((donor == order[0]) | (sink == order[0]) | (lengths[sink] == 0), 0, jnp.maximum(margin, 0))
    passed = jax.random.randint(jax.random.fold_in(own, 4), (number_of // 2,), 0, 1 << 20) % (margin + 1)
    lengths = lengths.at[donor].add(-passed).at[sink].add(passed)
    members = jnp.searchsorted(jnp.cumsum(lengths), jnp.arange(rows * top), side="right").astype(jnp.int32)
    grid = members.reshape(top, rows).T
    grid = grid[jax.random.permutation(jax.random.fold_in(own, 1), rows)]
    turn = jax.random.randint(jax.random.fold_in(own, 2), (rows, 1), 0, top)
    return jnp.take_along_axis(grid, (jnp.arange(top)[None, :] + turn) % top, axis=1)


def portions_of(amount, total, reach, skew, full):
    loads = [(1 << 20) // math.isqrt(grade ** skew) + 1 for grade in range(1, amount + 1)]
    largest = reach if full else min(reach, max(-(-total // amount), total * loads[0] // sum(loads)))
    least = 1 if total - largest >= amount - 1 else 0
    counts, surplus = [largest] + [least] * (amount - 1), total - largest - least * (amount - 1)
    while surplus > 0:
        free = [i for i in range(1, amount) if counts[i] < largest] or [i for i in range(1, amount) if counts[i] < reach]
        mass, left = sum([loads[i] for i in free]), surplus
        for i in free:
            addition = min(reach - counts[i], max(1, left * loads[i] // mass), surplus)
            counts[i] = counts[i] + addition
            surplus = surplus - addition
    return np.array(counts)


def centred(stream_key, dims, scale, most, cuts=(), kind=jnp.bfloat16):
    factor_of = block_scale(stream_key, dims, cuts, -0.22, 0.18) if cuts else 1.0
    result = jax.random.normal(stream_key, dims, jnp.float32) * scale * factor_of
    return jnp.minimum(jnp.maximum(result, -most), most).astype(kind)


def setup_inputs(seed: int = 0) -> dict:
    key_of = jax.random.split(jax.random.key(seed), 12)
    tokens = draw_tokens(jax.random.fold_in(key_of[11], 71), 0)
    ln_gain = draw_ln_gain(jax.random.fold_in(key_of[11], 71), 0)
    ln_bias = centred(key_of[2], (D,), 0.5, 3.0, (), jnp.float32)
    w_qkv = centred(key_of[3], (3, D, D), D ** -0.5, 0.15625, ((2, 4),))
    b_qkv = centred(key_of[4], (3, D), 0.5, 3.0, ((1, 4),), jnp.float32)
    w_out = centred(key_of[5], (D, D), D ** -0.5, 0.15625, ((0, 4),))
    b_out = centred(key_of[6], (D,), 0.5, 3.0, (), jnp.float32)
    merge_gain = jnp.clip(1.0 + 0.15 * jax.random.normal(key_of[7], (D,), jnp.float32), 0.25, 1.75)
    merge_bias = centred(key_of[8], (D,), 0.5, 3.0, (), jnp.float32)
    segments = jnp.searchsorted(jnp.cumsum(ragged(key_of[9], IMAGES, GROUPS, SPAN * TOK_DEV // 4, 2)), jnp.arange(GROUPS), side="right").astype(jnp.int32)
    owners_keys = jax.random.split(jax.random.fold_in(key_of[10], 1), GROUPS // MER_DEV)
    owners_turns = jax.random.permutation(jax.random.fold_in(key_of[10], 3), GROUPS // MER_DEV)
    owners = jax.vmap(lambda own, number: assign_block(jax.random.fold_in(key_of[10], 2), own, number, MER_DEV, N_SEQ, 1, CAP, 2))(owners_keys, owners_turns).reshape((GROUPS, 1))
    return dict(tokens=tokens, ln_gain=ln_gain, ln_bias=ln_bias, w_qkv=w_qkv, b_qkv=b_qkv, w_out=w_out, b_out=b_out, merge_gain=merge_gain, merge_bias=merge_bias, segments=segments, owners=owners)


epsilon = 1e-06
masked_score = -1e+30

def layer_norm(values, gain_row, shift_row):
    center = lax.optimization_barrier(jnp.mean(values, axis=-1, keepdims=True))
    centered = values - center
    spread = lax.optimization_barrier(jnp.mean(centered * centered, axis=-1, keepdims=True))
    return centered * lax.rsqrt(spread + epsilon) * gain_row + shift_row

def reference(tokens, ln_gain, ln_bias, w_qkv, b_qkv, w_out, b_out, merge_gain, merge_bias, segments, owners):
    normed = layer_norm(tokens.astype(jnp.float32), ln_gain, ln_bias).astype(jnp.bfloat16)
    projected = []
    for part_index in range(3):
        rows_out = jnp.dot(normed, w_qkv[part_index], preferred_element_type=jnp.float32) + b_qkv[part_index]
        projected.append(lax.optimization_barrier(rows_out.astype(jnp.bfloat16)))
    query, key_rows, value_rows = projected
    reach_rows = SPAN * TOK_DEV
    window_rows = 2 * reach_rows + TOK_DEV
    token_segment = jnp.repeat(segments, 4).astype(jnp.int32)
    padding = jnp.full((reach_rows,), -1, jnp.int32)
    padded_segment = jnp.concatenate([padding, token_segment, padding])
    padded_keys = jnp.pad(key_rows, ((reach_rows, reach_rows), (0, 0)))
    padded_values = jnp.pad(value_rows, ((reach_rows, reach_rows), (0, 0)))
    scale_factor = HEAD_DIM ** (-0.5)

    def one_block(block_index):
        row_start = (block_index * TOK_DEV).astype(jnp.int32)
        query_heads = lax.dynamic_slice_in_dim(query, row_start, TOK_DEV, 0).astype(jnp.float32).reshape(TOK_DEV, HEADS, HEAD_DIM)
        key_heads = lax.dynamic_slice_in_dim(padded_keys, row_start, window_rows, 0).astype(jnp.float32).reshape(window_rows, HEADS, HEAD_DIM)
        value_heads = lax.dynamic_slice_in_dim(padded_values, row_start, window_rows, 0).astype(jnp.float32).reshape(window_rows, HEADS, HEAD_DIM)
        query_segment = lax.dynamic_slice_in_dim(token_segment, row_start, TOK_DEV)
        key_segment = lax.dynamic_slice_in_dim(padded_segment, row_start, window_rows)
        scores = jnp.einsum('qhd,khd->hqk', query_heads, key_heads) * scale_factor
        allowed = query_segment[:, None] == key_segment[None, :]
        scores = jnp.where(allowed[None], scores, masked_score)
        row_top = lax.optimization_barrier(jnp.max(scores, axis=-1, keepdims=True))
        weights = jnp.exp(scores - row_top)
        totals = lax.optimization_barrier(jnp.sum(weights, axis=-1, keepdims=True))
        rounded = lax.optimization_barrier(weights.astype(jnp.bfloat16)).astype(jnp.float32)
        summed = jnp.einsum('hqk,khd->hqd', rounded, value_heads)
        return jnp.transpose(summed / totals, (1, 0, 2)).reshape(TOK_DEV, HEADS * HEAD_DIM).astype(jnp.bfloat16)
    attended = lax.map(one_block, jnp.arange(N_SEQ, dtype=jnp.int32)).reshape(TOKENS, D)
    group_width = D // N_TP
    head_total = jnp.zeros((TOKENS, D), jnp.float32)
    for group_index in range(N_TP):
        lower = group_index * group_width
        term = jnp.dot(attended[:, lower:lower + group_width], w_out[lower:lower + group_width], preferred_element_type=jnp.float32)
        head_total = head_total + lax.optimization_barrier(term.astype(jnp.bfloat16)).astype(jnp.float32)
    residual = tokens.astype(jnp.float32) + head_total + b_out
    merged = layer_norm(residual, merge_gain, merge_bias).astype(jnp.bfloat16).reshape(GROUPS, 4 * D)
    owner_rows = owners[:, 0].astype(jnp.int32).reshape(N_SEQ, MER_DEV)
    owner_table = (owner_rows[:, :, None] == jnp.arange(N_SEQ, dtype=jnp.int32)[None, None, :]).astype(jnp.int32)
    earlier = jnp.cumsum(owner_table, axis=1) - owner_table
    row_slot = lax.optimization_barrier(jnp.sum(earlier * owner_table, axis=2))
    source_index = jnp.arange(N_SEQ, dtype=jnp.int32)[:, None]
    target_row = (owner_rows * (N_SEQ * CAP) + source_index * CAP + row_slot).astype(jnp.int32).reshape(GROUPS)
    routed = jnp.zeros((N_SEQ * N_SEQ * CAP, 4 * D), jnp.bfloat16).at[target_row].set(merged)
    return routed
```

```python
import jax
import jax.numpy as jnp
from jax import lax
from jax.sharding import PartitionSpec as P

HEAD_DIM = 80
SPAN = 4


epsilon = 1e-06
masked_score = -1e30


def from_behind(value, axis, steps):
    count = lax.axis_size(axis)
    leading, last = (max(0, -steps), min(count, count - steps))
    return lax.ppermute(value, axis, [(source, source + steps) for source in range(leading, last)])


def layer_norm(values, gain_row, shift_row):
    center = jnp.mean(values, axis=-1, keepdims=True)
    centered = values - center
    spread = jnp.mean(centered * centered, axis=-1, keepdims=True)
    return centered * lax.rsqrt(spread + epsilon) * gain_row + shift_row


def per_device(
    tokens, ln_gain, ln_bias, w_qkv, b_qkv, w_out, b_out, merge_gain, merge_bias, segments, owners
):
    tok_dev = tokens.shape[0]
    model_width = tokens.shape[1]
    local_width = w_qkv.shape[2]
    local_heads = local_width // HEAD_DIM
    seq_count = lax.axis_size("seq")
    seq_index = lax.axis_index("seq")
    row_start = seq_index * tok_dev
    reach_rows = SPAN * tok_dev
    scale_factor = HEAD_DIM ** (-0.5)
    normed = layer_norm(tokens.astype(jnp.float32), ln_gain, ln_bias).astype(jnp.bfloat16)
    query = (jnp.dot(normed, w_qkv[0], preferred_element_type=jnp.float32) + b_qkv[0]).astype(
        jnp.bfloat16
    )
    key_rows = (jnp.dot(normed, w_qkv[1], preferred_element_type=jnp.float32) + b_qkv[1]).astype(
        jnp.bfloat16
    )
    value_rows = (jnp.dot(normed, w_qkv[2], preferred_element_type=jnp.float32) + b_qkv[2]).astype(
        jnp.bfloat16
    )
    key_value = jnp.concatenate([key_rows, value_rows], axis=1)
    group_rows = tok_dev // 4
    reach_groups = SPAN * group_rows
    padding = jnp.full((reach_groups,), -1, jnp.int32)
    padded_segment = jnp.concatenate([padding, segments, padding])

    def segment_window(key_start, length):
        groups = lax.dynamic_slice_in_dim(padded_segment, key_start // 4 + reach_groups, length // 4)
        return jnp.repeat(groups, 4)

    query_segment = segment_window(row_start, tok_dev)
    query_heads = query.reshape(tok_dev, local_heads, HEAD_DIM)

    def block_scores(block, key_segment):
        key_heads = block[:, :local_width].reshape(-1, local_heads, HEAD_DIM)
        value_heads = block[:, local_width:].reshape(-1, local_heads, HEAD_DIM)
        scores = (
            jnp.einsum("qhd,khd->hqk", query_heads, key_heads, preferred_element_type=jnp.float32)
            * scale_factor
        )
        allowed = query_segment[:, None] == key_segment[None, :]
        return (jnp.where(allowed[None], scores, masked_score), value_heads)

    def absorb(state, block, key_segment):
        row_top, totals, summed = state
        scores, value_heads = block_scores(block, key_segment)
        new_top = jnp.maximum(row_top, jnp.max(scores, axis=-1, keepdims=True))
        factor = jnp.exp(row_top - new_top)
        weights = jnp.exp(scores - new_top)
        totals = totals * factor + jnp.sum(weights, axis=-1, keepdims=True)
        summed = summed * factor + jnp.einsum(
            "hqk,khd->hqd",
            weights.astype(jnp.bfloat16),
            value_heads,
            preferred_element_type=jnp.float32,
        )
        return (new_top, totals, summed)

    def absorb_remote(state, block, key_start):
        key_segment = segment_window(key_start, tok_dev)
        return absorb(state, block, key_segment)

    start_state = (
        jnp.full((local_heads, tok_dev, 1), masked_score, jnp.float32),
        jnp.zeros((local_heads, tok_dev, 1), jnp.float32),
        jnp.zeros((local_heads, tok_dev, HEAD_DIM), jnp.float32),
    )
    state = absorb(start_state, key_value, query_segment)
    below = key_value
    above = key_value
    for distance in range(1, SPAN + 1):
        below = from_behind(below, "seq", 1)
        above = from_behind(above, "seq", -1)
        state = absorb_remote(state, below, row_start - distance * tok_dev)
        state = absorb_remote(state, above, row_start + distance * tok_dev)
    row_top, totals, summed = state
    tp_index = lax.axis_index("tp")
    quarter = tok_dev // 4
    by_token = (summed / totals).reshape(local_heads, quarter, 4, HEAD_DIM)
    attended = jnp.transpose(by_token, (2, 1, 0, 3)).reshape(4, quarter, local_width).astype(jnp.bfloat16)
    head_term = jnp.einsum(
        "tgc,cd->tgd", attended, w_out, preferred_element_type=jnp.float32
    ).astype(jnp.bfloat16)
    head_terms = lax.all_to_all(head_term, "tp", split_axis=0, concat_axis=0, tiled=True)
    head_total = jnp.sum(head_terms.astype(jnp.float32), axis=0)
    own_tokens = lax.dynamic_index_in_dim(
        tokens.reshape(quarter, 4, model_width), tp_index, 1, keepdims=False
    )
    own_rows = own_tokens.astype(jnp.float32) + head_total + b_out
    merged_rows = layer_norm(own_rows, merge_gain, merge_bias).astype(jnp.bfloat16)
    owner_rows = owners[:, 0]
    capacity = max(2, 2 * quarter // seq_count)
    owner_table = (owner_rows[:, None] == jnp.arange(seq_count, dtype=jnp.int32)[None, :]).astype(
        jnp.int32
    )
    earlier = jnp.cumsum(owner_table, axis=0) - owner_table
    row_slot = jnp.sum(earlier * owner_table, axis=1)
    target_row = owner_rows * capacity + row_slot
    placing = (
        jnp.arange(seq_count * capacity, dtype=jnp.int32)[:, None] == target_row[None, :]
    ).astype(jnp.bfloat16)
    outgoing = jnp.dot(placing, merged_rows, preferred_element_type=jnp.float32).astype(
        jnp.bfloat16
    )
    return lax.all_to_all(outgoing, "seq", split_axis=0, concat_axis=0, tiled=True)


def solution(mesh):
    placed = (
        P("seq", None),
        P(),
        P(),
        P(None, None, "tp"),
        P(None, "tp"),
        P("tp", None),
        P(),
        P(),
        P(),
        P(),
        P("seq", None),
    )
    return jax.shard_map(
        per_device, mesh=mesh, in_specs=placed, out_specs=P("seq", "tp"), check_vma=False
    )
```

```python
import jax
import jax.numpy as jnp
from jax import lax
from jax.sharding import PartitionSpec as P

HEAD_DIM = 80
SPAN = 4


epsilon = 1e-06
masked_score = -1e30


def from_behind(value, axis, steps):
    count = lax.axis_size(axis)
    leading, last = (max(0, -steps), min(count, count - steps))
    return lax.ppermute(value, axis, [(source, source + steps) for source in range(leading, last)])


def layer_norm(values, gain_row, shift_row):
    center = jnp.mean(values, axis=-1, keepdims=True)
    centered = values - center
    spread = jnp.mean(centered * centered, axis=-1, keepdims=True)
    return centered * lax.rsqrt(spread + epsilon) * gain_row + shift_row


def per_device(
    tokens, ln_gain, ln_bias, w_qkv, b_qkv, w_out, b_out, merge_gain, merge_bias, segments, owners
):
    tok_dev = tokens.shape[0]
    model_width = tokens.shape[1]
    local_width = w_qkv.shape[2]
    local_heads = local_width // HEAD_DIM
    seq_count = lax.axis_size("seq")
    seq_index = lax.axis_index("seq")
    row_start = seq_index * tok_dev
    reach_rows = SPAN * tok_dev
    scale_factor = HEAD_DIM ** (-0.5)
    normed = layer_norm(tokens.astype(jnp.float32), ln_gain, ln_bias).astype(jnp.bfloat16)
    query = (jnp.dot(normed, w_qkv[0], preferred_element_type=jnp.float32) + b_qkv[0]).astype(
        jnp.bfloat16
    )
    key_rows = (jnp.dot(normed, w_qkv[1], preferred_element_type=jnp.float32) + b_qkv[1]).astype(
        jnp.bfloat16
    )
    value_rows = (jnp.dot(normed, w_qkv[2], preferred_element_type=jnp.float32) + b_qkv[2]).astype(
        jnp.bfloat16
    )
    key_value = jnp.concatenate([key_rows, value_rows], axis=1)
    group_rows = tok_dev // 4
    reach_groups = SPAN * group_rows
    padding = jnp.full((reach_groups,), -1, jnp.int32)
    padded_segment = jnp.concatenate([padding, segments, padding])

    def segment_window(key_start, length):
        groups = lax.dynamic_slice_in_dim(padded_segment, key_start // 4 + reach_groups, length // 4)
        return jnp.repeat(groups, 4)

    query_segment = segment_window(row_start, tok_dev)
    query_heads = query.reshape(tok_dev, local_heads, HEAD_DIM)

    def block_scores(block, key_segment):
        key_heads = block[:, :local_width].reshape(-1, local_heads, HEAD_DIM)
        value_heads = block[:, local_width:].reshape(-1, local_heads, HEAD_DIM)
        scores = (
            jnp.einsum("qhd,khd->hqk", query_heads, key_heads, preferred_element_type=jnp.float32)
            * scale_factor
        )
        allowed = query_segment[:, None] == key_segment[None, :]
        return (jnp.where(allowed[None], scores, masked_score), value_heads)

    def absorb(state, block, key_segment):
        row_top, totals, summed = state
        scores, value_heads = block_scores(block, key_segment)
        new_top = jnp.maximum(row_top, jnp.max(scores, axis=-1, keepdims=True))
        factor = jnp.exp(row_top - new_top)
        weights = jnp.exp(scores - new_top)
        totals = totals * factor + jnp.sum(weights, axis=-1, keepdims=True)
        summed = summed * factor + jnp.einsum(
            "hqk,khd->hqd",
            weights.astype(jnp.bfloat16),
            value_heads,
            preferred_element_type=jnp.float32,
        )
        return (new_top, totals, summed)

    def absorb_remote(state, block, key_start):
        key_segment = segment_window(key_start, tok_dev)
        return absorb(state, block, key_segment)

    start_state = (
        jnp.full((local_heads, tok_dev, 1), masked_score, jnp.float32),
        jnp.zeros((local_heads, tok_dev, 1), jnp.float32),
        jnp.zeros((local_heads, tok_dev, HEAD_DIM), jnp.float32),
    )
    sign = 1 - 2 * (seq_index % 2)

    def swap(value):
        return lax.ppermute(value, "seq", [(i, i ^ 1) for i in range(seq_count)])

    def absorb_at(state, block, offset):
        return absorb_remote(state, block, row_start + offset * tok_dev)

    below_2 = from_behind(key_value, "seq", 2)
    above_2 = from_behind(key_value, "seq", -2)
    partner_own = swap(key_value)
    state = absorb(start_state, key_value, query_segment)
    below_4 = from_behind(below_2, "seq", 2)
    above_4 = from_behind(above_2, "seq", -2)
    partner_near = swap(jnp.concatenate([below_2, above_2], axis=0))
    state = absorb_at(state, partner_own, sign)
    state = absorb_at(state, below_2, -2)
    state = absorb_at(state, above_2, 2)
    state = absorb_at(state, partner_near[:tok_dev], sign - 2)
    state = absorb_at(state, partner_near[tok_dev:], sign + 2)
    partner_far = swap(jnp.where(sign > 0, above_4, below_4))
    state = absorb_at(state, below_4, -4)
    state = absorb_at(state, above_4, 4)
    state = absorb_at(state, partner_far, -3 * sign)
    row_top, totals, summed = state
    tp_index = lax.axis_index("tp")
    quarter = tok_dev // 4
    by_token = (summed / totals).reshape(local_heads, quarter, 4, HEAD_DIM)
    attended = jnp.transpose(by_token, (2, 1, 0, 3)).reshape(4, quarter, local_width).astype(jnp.bfloat16)
    head_term = jnp.einsum(
        "tgc,cd->tgd", attended, w_out, preferred_element_type=jnp.float32
    ).astype(jnp.bfloat16)
    head_terms = lax.all_to_all(head_term, "tp", split_axis=0, concat_axis=0, tiled=True)
    head_total = jnp.sum(head_terms.astype(jnp.float32), axis=0)
    own_tokens = lax.dynamic_index_in_dim(
        tokens.reshape(quarter, 4, model_width), tp_index, 1, keepdims=False
    )
    own_rows = own_tokens.astype(jnp.float32) + head_total + b_out
    merged_rows = layer_norm(own_rows, merge_gain, merge_bias).astype(jnp.bfloat16)
    owner_rows = owners[:, 0]
    capacity = max(2, 2 * quarter // seq_count)
    owner_table = (owner_rows[:, None] == jnp.arange(seq_count, dtype=jnp.int32)[None, :]).astype(
        jnp.int32
    )
    earlier = jnp.cumsum(owner_table, axis=0) - owner_table
    row_slot = jnp.sum(earlier * owner_table, axis=1)
    target_row = owner_rows * capacity + row_slot
    placing = (
        jnp.arange(seq_count * capacity, dtype=jnp.int32)[:, None] == target_row[None, :]
    ).astype(jnp.bfloat16)
    outgoing = jnp.dot(placing, merged_rows, preferred_element_type=jnp.float32).astype(
        jnp.bfloat16
    )
    return lax.all_to_all(outgoing, "seq", split_axis=0, concat_axis=0, tiled=True)


def solution(mesh):
    placed = (
        P("seq", None),
        P(),
        P(),
        P(None, None, "tp"),
        P(None, "tp"),
        P("tp", None),
        P(),
        P(),
        P(),
        P(),
        P("seq", None),
    )
    return jax.shard_map(
        per_device, mesh=mesh, in_specs=placed, out_specs=P("seq", "tp"), check_vma=False
    )
```

```python
import jax
import jax.numpy as jnp
from jax import lax
from jax.sharding import PartitionSpec as P

HEAD_DIM = 80
SPAN = 4


epsilon = 1e-06
masked_score = -1e30


def from_behind(value, axis, steps):
    count = lax.axis_size(axis)
    leading, last = (max(0, -steps), min(count, count - steps))
    return lax.ppermute(value, axis, [(source, source + steps) for source in range(leading, last)])


def layer_norm(values, gain_row, shift_row):
    center = jnp.mean(values, axis=-1, keepdims=True)
    centered = values - center
    spread = jnp.mean(centered * centered, axis=-1, keepdims=True)
    return centered * lax.rsqrt(spread + epsilon) * gain_row + shift_row


def per_device(
    tokens, ln_gain, ln_bias, w_qkv, b_qkv, w_out, b_out, merge_gain, merge_bias, segments, owners
):
    tok_dev = tokens.shape[0]
    model_width = tokens.shape[1]
    local_width = w_qkv.shape[2]
    local_heads = local_width // HEAD_DIM
    seq_count = lax.axis_size("seq")
    seq_index = lax.axis_index("seq")
    row_start = seq_index * tok_dev
    reach_rows = SPAN * tok_dev
    scale_factor = HEAD_DIM ** (-0.5)
    normed = layer_norm(tokens.astype(jnp.float32), ln_gain, ln_bias).astype(jnp.bfloat16)
    query = (jnp.dot(normed, w_qkv[0], preferred_element_type=jnp.float32) + b_qkv[0]).astype(
        jnp.bfloat16
    )
    key_rows = (jnp.dot(normed, w_qkv[1], preferred_element_type=jnp.float32) + b_qkv[1]).astype(
        jnp.bfloat16
    )
    value_rows = (jnp.dot(normed, w_qkv[2], preferred_element_type=jnp.float32) + b_qkv[2]).astype(
        jnp.bfloat16
    )
    key_value = jnp.concatenate([key_rows, value_rows], axis=1)
    group_rows = tok_dev // 4
    reach_groups = SPAN * group_rows
    padding = jnp.full((reach_groups,), -1, jnp.int32)
    padded_segment = jnp.concatenate([padding, segments, padding])

    def segment_window(key_start, length):
        groups = lax.dynamic_slice_in_dim(padded_segment, key_start // 4 + reach_groups, length // 4)
        return jnp.repeat(groups, 4)

    query_segment = segment_window(row_start, tok_dev)
    query_heads = query.reshape(tok_dev, local_heads, HEAD_DIM)

    def block_scores(block, key_segment):
        key_heads = block[:, :local_width].reshape(-1, local_heads, HEAD_DIM)
        value_heads = block[:, local_width:].reshape(-1, local_heads, HEAD_DIM)
        scores = (
            jnp.einsum("qhd,khd->hqk", query_heads, key_heads, preferred_element_type=jnp.float32)
            * scale_factor
        )
        allowed = query_segment[:, None] == key_segment[None, :]
        return (jnp.where(allowed[None], scores, masked_score), value_heads)

    def absorb(state, block, key_segment):
        row_top, totals, summed = state
        scores, value_heads = block_scores(block, key_segment)
        new_top = jnp.maximum(row_top, jnp.max(scores, axis=-1, keepdims=True))
        factor = jnp.exp(row_top - new_top)
        weights = jnp.exp(scores - new_top)
        totals = totals * factor + jnp.sum(weights, axis=-1, keepdims=True)
        summed = summed * factor + jnp.einsum(
            "hqk,khd->hqd",
            weights.astype(jnp.bfloat16),
            value_heads,
            preferred_element_type=jnp.float32,
        )
        return (new_top, totals, summed)

    def absorb_remote(state, block, key_start):
        key_segment = segment_window(key_start, tok_dev)
        return absorb(state, block, key_segment)

    start_state = (
        jnp.full((local_heads, tok_dev, 1), masked_score, jnp.float32),
        jnp.zeros((local_heads, tok_dev, 1), jnp.float32),
        jnp.zeros((local_heads, tok_dev, HEAD_DIM), jnp.float32),
    )
    sign = 1 - 2 * (seq_index % 2)

    def swap(value):
        return lax.ppermute(value, "seq", [(i, i ^ 1) for i in range(seq_count)])

    def absorb_at(state, block, offset):
        return absorb_remote(state, block, row_start + offset * tok_dev)

    below_2 = from_behind(key_value, "seq", 2)
    above_2 = from_behind(key_value, "seq", -2)
    below_4 = from_behind(key_value, "seq", 4)
    above_4 = from_behind(key_value, "seq", -4)
    partner_own = swap(key_value)
    state = absorb(start_state, key_value, query_segment)
    partner_rest = swap(jnp.concatenate([below_2, above_2, jnp.where(sign > 0, above_4, below_4)], axis=0))
    state = absorb_at(state, partner_own, sign)
    state = absorb_at(state, below_2, -2)
    state = absorb_at(state, above_2, 2)
    state = absorb_at(state, below_4, -4)
    state = absorb_at(state, above_4, 4)
    state = absorb_at(state, partner_rest[:tok_dev], sign - 2)
    state = absorb_at(state, partner_rest[tok_dev : 2 * tok_dev], sign + 2)
    state = absorb_at(state, partner_rest[2 * tok_dev :], -3 * sign)
    row_top, totals, summed = state
    tp_index = lax.axis_index("tp")
    quarter = tok_dev // 4
    by_token = (summed / totals).reshape(local_heads, quarter, 4, HEAD_DIM)
    attended = jnp.transpose(by_token, (2, 1, 0, 3)).reshape(4, quarter, local_width).astype(jnp.bfloat16)
    head_term = jnp.einsum(
        "tgc,cd->tgd", attended, w_out, preferred_element_type=jnp.float32
    ).astype(jnp.bfloat16)
    head_terms = lax.all_to_all(head_term, "tp", split_axis=0, concat_axis=0, tiled=True)
    head_total = jnp.sum(head_terms.astype(jnp.float32), axis=0)
    own_tokens = lax.dynamic_index_in_dim(
        tokens.reshape(quarter, 4, model_width), tp_index, 1, keepdims=False
    )
    own_rows = own_tokens.astype(jnp.float32) + head_total + b_out
    merged_rows = layer_norm(own_rows, merge_gain, merge_bias).astype(jnp.bfloat16)
    owner_rows = owners[:, 0]
    capacity = max(2, 2 * quarter // seq_count)
    owner_table = (owner_rows[:, None] == jnp.arange(seq_count, dtype=jnp.int32)[None, :]).astype(
        jnp.int32
    )
    earlier = jnp.cumsum(owner_table, axis=0) - owner_table
    row_slot = jnp.sum(earlier * owner_table, axis=1)
    target_row = owner_rows * capacity + row_slot
    placing = (
        jnp.arange(seq_count * capacity, dtype=jnp.int32)[:, None] == target_row[None, :]
    ).astype(jnp.bfloat16)
    outgoing = jnp.dot(placing, merged_rows, preferred_element_type=jnp.float32).astype(
        jnp.bfloat16
    )
    return lax.all_to_all(outgoing, "seq", split_axis=0, concat_axis=0, tiled=True)


def solution(mesh):
    placed = (
        P("seq", None),
        P(),
        P(),
        P(None, None, "tp"),
        P(None, "tp"),
        P("tp", None),
        P(),
        P(),
        P(),
        P(),
        P("seq", None),
    )
    return jax.shard_map(
        per_device, mesh=mesh, in_specs=placed, out_specs=P("seq", "tp"), check_vma=False
    )
```

```python
import jax
import jax.numpy as jnp
from jax import lax
from jax.sharding import PartitionSpec as P

HEAD_DIM = 80
SPAN = 4


epsilon = 1e-06
masked_score = -1e30


def from_behind(value, axis, steps):
    count = lax.axis_size(axis)
    leading, last = (max(0, -steps), min(count, count - steps))
    return lax.ppermute(value, axis, [(source, source + steps) for source in range(leading, last)])


def layer_norm(values, gain_row, shift_row):
    center = jnp.mean(values, axis=-1, keepdims=True)
    centered = values - center
    spread = jnp.mean(centered * centered, axis=-1, keepdims=True)
    return centered * lax.rsqrt(spread + epsilon) * gain_row + shift_row


def per_device(
    tokens, ln_gain, ln_bias, w_qkv, b_qkv, w_out, b_out, merge_gain, merge_bias, segments, owners
):
    tok_dev = tokens.shape[0]
    model_width = tokens.shape[1]
    local_width = w_qkv.shape[2]
    local_heads = local_width // HEAD_DIM
    seq_count = lax.axis_size("seq")
    seq_index = lax.axis_index("seq")
    row_start = seq_index * tok_dev
    reach_rows = SPAN * tok_dev
    scale_factor = HEAD_DIM ** (-0.5)
    normed = layer_norm(tokens.astype(jnp.float32), ln_gain, ln_bias).astype(jnp.bfloat16)
    query = (jnp.dot(normed, w_qkv[0], preferred_element_type=jnp.float32) + b_qkv[0]).astype(
        jnp.bfloat16
    )
    key_value = (
        jnp.einsum("tc,kcd->tkd", normed, w_qkv[1:], preferred_element_type=jnp.float32) + b_qkv[1:]
    ).astype(jnp.bfloat16).reshape(tok_dev, 2 * local_width)
    group_rows = tok_dev // 4
    reach_groups = SPAN * group_rows
    padding = jnp.full((reach_groups,), -1, jnp.int32)
    padded_segment = jnp.concatenate([padding, segments, padding])

    def segment_window(key_start, length):
        groups = lax.dynamic_slice_in_dim(padded_segment, key_start // 4 + reach_groups, length // 4)
        return jnp.repeat(groups, 4)

    query_segment = segment_window(row_start, tok_dev)
    query_heads = query.reshape(tok_dev, local_heads, HEAD_DIM)

    def block_scores(block, key_segment):
        key_heads = block[:, :local_width].reshape(-1, local_heads, HEAD_DIM)
        value_heads = block[:, local_width:].reshape(-1, local_heads, HEAD_DIM)
        scores = (
            jnp.einsum("qhd,khd->hqk", query_heads, key_heads, preferred_element_type=jnp.float32)
            * scale_factor
        )
        allowed = query_segment[:, None] == key_segment[None, :]
        return (jnp.where(allowed[None], scores, masked_score), value_heads)

    def absorb(state, block, key_segment):
        row_top, totals, summed = state
        scores, value_heads = block_scores(block, key_segment)
        new_top = jnp.maximum(row_top, jnp.max(scores, axis=-1, keepdims=True))
        factor = jnp.exp(row_top - new_top)
        weights = jnp.exp(scores - new_top)
        totals = totals * factor + jnp.sum(weights, axis=-1, keepdims=True)
        summed = summed * factor + jnp.einsum(
            "hqk,khd->hqd",
            weights.astype(jnp.bfloat16),
            value_heads,
            preferred_element_type=jnp.float32,
        )
        return (new_top, totals, summed)

    def absorb_remote(state, block, key_start):
        key_segment = segment_window(key_start, tok_dev)
        return absorb(state, block, key_segment)

    start_state = (
        jnp.full((local_heads, tok_dev, 1), masked_score, jnp.float32),
        jnp.zeros((local_heads, tok_dev, 1), jnp.float32),
        jnp.zeros((local_heads, tok_dev, HEAD_DIM), jnp.float32),
    )
    sign = 1 - 2 * (seq_index % 2)

    def swap(value):
        return lax.ppermute(value, "seq", [(i, i ^ 1) for i in range(seq_count)])

    def absorb_at(state, block, offset):
        return absorb_remote(state, block, row_start + offset * tok_dev)

    below_2 = from_behind(key_value, "seq", 2)
    above_2 = from_behind(key_value, "seq", -2)
    below_4 = from_behind(key_value, "seq", 4)
    above_4 = from_behind(key_value, "seq", -4)
    partner_own = swap(key_value)
    state = absorb(start_state, key_value, query_segment)
    partner_near = swap(jnp.concatenate([below_2, above_2], axis=0))
    partner_far = swap(jnp.where(sign > 0, above_4, below_4))
    state = absorb_at(state, partner_own, sign)
    state = absorb_at(state, below_2, -2)
    state = absorb_at(state, above_2, 2)
    state = absorb_at(state, partner_near[:tok_dev], sign - 2)
    state = absorb_at(state, partner_near[tok_dev:], sign + 2)
    state = absorb_at(state, below_4, -4)
    state = absorb_at(state, above_4, 4)
    state = absorb_at(state, partner_far, -3 * sign)
    row_top, totals, summed = state
    tp_index = lax.axis_index("tp")
    quarter = tok_dev // 4
    by_token = (summed / totals).reshape(local_heads, quarter, 4, HEAD_DIM)
    attended = jnp.transpose(by_token, (2, 1, 0, 3)).reshape(4, quarter, local_width).astype(jnp.bfloat16)
    head_term = jnp.einsum(
        "tgc,cd->tgd", attended, w_out, preferred_element_type=jnp.float32
    ).astype(jnp.bfloat16)
    head_terms = lax.all_to_all(head_term, "tp", split_axis=0, concat_axis=0, tiled=True)
    head_total = jnp.sum(head_terms.astype(jnp.float32), axis=0)
    own_tokens = lax.dynamic_index_in_dim(
        tokens.reshape(quarter, 4, model_width), tp_index, 1, keepdims=False
    )
    own_rows = own_tokens.astype(jnp.float32) + head_total + b_out
    merged_rows = layer_norm(own_rows, merge_gain, merge_bias).astype(jnp.bfloat16)
    owner_rows = owners[:, 0]
    capacity = max(2, 2 * quarter // seq_count)
    owner_table = (owner_rows[:, None] == jnp.arange(seq_count, dtype=jnp.int32)[None, :]).astype(
        jnp.int32
    )
    earlier = jnp.cumsum(owner_table, axis=0) - owner_table
    row_slot = jnp.sum(earlier * owner_table, axis=1)
    target_row = owner_rows * capacity + row_slot
    placing = (
        jnp.arange(seq_count * capacity, dtype=jnp.int32)[:, None] == target_row[None, :]
    ).astype(jnp.bfloat16)
    outgoing = jnp.dot(placing, merged_rows, preferred_element_type=jnp.float32).astype(
        jnp.bfloat16
    )
    return lax.all_to_all(outgoing, "seq", split_axis=0, concat_axis=0, tiled=True)


def solution(mesh):
    placed = (
        P("seq", None),
        P(),
        P(),
        P(None, None, "tp"),
        P(None, "tp"),
        P("tp", None),
        P(),
        P(),
        P(),
        P(),
        P("seq", None),
    )
    return jax.shard_map(
        per_device, mesh=mesh, in_specs=placed, out_specs=P("seq", "tp"), check_vma=False
    )
```

```python
import jax
import jax.numpy as jnp
from jax import lax
from jax.sharding import PartitionSpec as P

HEAD_DIM = 80
SPAN = 4


epsilon = 1e-06
masked_score = -1e30


def from_behind(value, axis, steps):
    count = lax.axis_size(axis)
    leading, last = (max(0, -steps), min(count, count - steps))
    return lax.ppermute(value, axis, [(source, source + steps) for source in range(leading, last)])


def layer_norm(values, gain_row, shift_row):
    center = jnp.mean(values, axis=-1, keepdims=True)
    centered = values - center
    spread = jnp.mean(centered * centered, axis=-1, keepdims=True)
    return centered * lax.rsqrt(spread + epsilon) * gain_row + shift_row


def per_device(
    tokens, ln_gain, ln_bias, w_qkv, b_qkv, w_out, b_out, merge_gain, merge_bias, segments, owners
):
    tok_dev = tokens.shape[0]
    model_width = tokens.shape[1]
    local_width = w_qkv.shape[2]
    local_heads = local_width // HEAD_DIM
    seq_count = lax.axis_size("seq")
    seq_index = lax.axis_index("seq")
    row_start = seq_index * tok_dev
    reach_rows = SPAN * tok_dev
    scale_factor = HEAD_DIM ** (-0.5)
    normed = layer_norm(tokens.astype(jnp.float32), ln_gain, ln_bias).astype(jnp.bfloat16)
    query = (jnp.dot(normed, w_qkv[0], preferred_element_type=jnp.float32) + b_qkv[0]).astype(
        jnp.bfloat16
    )
    key_value = (
        jnp.einsum("tc,kcd->tkd", normed, w_qkv[1:], preferred_element_type=jnp.float32) + b_qkv[1:]
    ).astype(jnp.bfloat16).reshape(tok_dev, 2 * local_width)
    group_rows = tok_dev // 4
    reach_groups = SPAN * group_rows
    padding = jnp.full((reach_groups,), -1, jnp.int32)
    padded_segment = jnp.concatenate([padding, segments, padding])

    window_segment = lax.optimization_barrier(
        jnp.repeat(
            lax.dynamic_slice_in_dim(padded_segment, seq_index * group_rows, (2 * SPAN + 1) * group_rows), 4
        )
    )

    def segment_window(key_start, length):
        return lax.dynamic_slice_in_dim(window_segment, key_start - row_start + reach_rows, length)

    query_segment = segment_window(row_start, tok_dev)
    query_heads = query.reshape(tok_dev, local_heads, HEAD_DIM)

    def block_scores(block, key_segment):
        key_heads = block[:, :local_width].reshape(-1, local_heads, HEAD_DIM)
        value_heads = block[:, local_width:].reshape(-1, local_heads, HEAD_DIM)
        scores = (
            jnp.einsum("qhd,khd->hqk", query_heads, key_heads, preferred_element_type=jnp.float32)
            * scale_factor
        )
        allowed = query_segment[:, None] == key_segment[None, :]
        return (jnp.where(allowed[None], scores, masked_score), value_heads)

    def absorb(state, block, key_segment):
        row_top, totals, summed = state
        scores, value_heads = block_scores(block, key_segment)
        new_top = jnp.maximum(row_top, jnp.max(scores, axis=-1, keepdims=True))
        factor = jnp.exp(row_top - new_top)
        weights = jnp.exp(scores - new_top)
        totals = totals * factor + jnp.sum(weights, axis=-1, keepdims=True)
        summed = summed * factor + jnp.einsum(
            "hqk,khd->hqd",
            weights.astype(jnp.bfloat16),
            value_heads,
            preferred_element_type=jnp.float32,
        )
        return (new_top, totals, summed)

    def absorb_remote(state, block, key_start):
        key_segment = segment_window(key_start, tok_dev)
        return absorb(state, block, key_segment)

    start_state = (
        jnp.full((local_heads, tok_dev, 1), masked_score, jnp.float32),
        jnp.zeros((local_heads, tok_dev, 1), jnp.float32),
        jnp.zeros((local_heads, tok_dev, HEAD_DIM), jnp.float32),
    )
    sign = 1 - 2 * (seq_index % 2)

    def swap(value):
        return lax.ppermute(value, "seq", [(i, i ^ 1) for i in range(seq_count)])

    def absorb_at(state, block, offset):
        return absorb_remote(state, block, row_start + offset * tok_dev)

    below_2 = from_behind(key_value, "seq", 2)
    above_2 = from_behind(key_value, "seq", -2)
    below_4 = from_behind(key_value, "seq", 4)
    above_4 = from_behind(key_value, "seq", -4)
    partner_own = swap(key_value)
    state = absorb(start_state, key_value, query_segment)
    partner_near = swap(jnp.concatenate([below_2, above_2], axis=0))
    partner_far = swap(jnp.where(sign > 0, above_4, below_4))
    state = absorb_at(state, partner_own, sign)
    state = absorb_at(state, below_2, -2)
    state = absorb_at(state, above_2, 2)
    state = absorb_at(state, partner_near[:tok_dev], sign - 2)
    state = absorb_at(state, partner_near[tok_dev:], sign + 2)
    state = absorb_at(state, below_4, -4)
    state = absorb_at(state, above_4, 4)
    state = absorb_at(state, partner_far, -3 * sign)
    row_top, totals, summed = state
    tp_index = lax.axis_index("tp")
    quarter = tok_dev // 4
    by_token = (summed / totals).reshape(local_heads, quarter, 4, HEAD_DIM)
    attended = jnp.transpose(by_token, (2, 1, 0, 3)).reshape(4, quarter, local_width).astype(jnp.bfloat16)
    head_term = jnp.einsum(
        "tgc,cd->tgd", attended, w_out, preferred_element_type=jnp.float32
    ).astype(jnp.bfloat16)
    head_terms = lax.all_to_all(head_term, "tp", split_axis=0, concat_axis=0, tiled=True)
    head_total = jnp.sum(head_terms.astype(jnp.float32), axis=0)
    own_tokens = lax.dynamic_index_in_dim(
        tokens.reshape(quarter, 4, model_width), tp_index, 1, keepdims=False
    )
    own_rows = own_tokens.astype(jnp.float32) + head_total + b_out
    merged_rows = layer_norm(own_rows, merge_gain, merge_bias).astype(jnp.bfloat16)
    owner_rows = owners[:, 0]
    capacity = max(2, 2 * quarter // seq_count)
    owner_table = (owner_rows[:, None] == jnp.arange(seq_count, dtype=jnp.int32)[None, :]).astype(
        jnp.int32
    )
    earlier = jnp.cumsum(owner_table, axis=0) - owner_table
    row_slot = jnp.sum(earlier * owner_table, axis=1)
    target_row = owner_rows * capacity + row_slot
    placing = (
        jnp.arange(seq_count * capacity, dtype=jnp.int32)[:, None] == target_row[None, :]
    ).astype(jnp.bfloat16)
    outgoing = jnp.dot(placing, merged_rows, preferred_element_type=jnp.float32).astype(
        jnp.bfloat16
    )
    return lax.all_to_all(outgoing, "seq", split_axis=0, concat_axis=0, tiled=True)


def solution(mesh):
    placed = (
        P("seq", None),
        P(),
        P(),
        P(None, None, "tp"),
        P(None, "tp"),
        P("tp", None),
        P(),
        P(),
        P(),
        P(),
        P("seq", None),
    )
    return jax.shard_map(
        per_device, mesh=mesh, in_specs=placed, out_specs=P("seq", "tp"), check_vma=False
    )
```

```python
import jax
import jax.numpy as jnp
from jax import lax
from jax.sharding import PartitionSpec as P

HEAD_DIM = 80
SPAN = 4


epsilon = 1e-06
masked_score = -1e30


def from_behind(value, axis, steps):
    count = lax.axis_size(axis)
    leading, last = (max(0, -steps), min(count, count - steps))
    return lax.ppermute(value, axis, [(source, source + steps) for source in range(leading, last)])


def layer_norm(values, gain_row, shift_row):
    center = jnp.mean(values, axis=-1, keepdims=True)
    centered = values - center
    spread = jnp.mean(centered * centered, axis=-1, keepdims=True)
    return centered * lax.rsqrt(spread + epsilon) * gain_row + shift_row


def per_device(
    tokens, ln_gain, ln_bias, w_qkv, b_qkv, w_out, b_out, merge_gain, merge_bias, segments, owners
):
    tok_dev = tokens.shape[0]
    model_width = tokens.shape[1]
    local_width = w_qkv.shape[2]
    local_heads = local_width // HEAD_DIM
    seq_count = lax.axis_size("seq")
    seq_index = lax.axis_index("seq")
    row_start = seq_index * tok_dev
    reach_rows = SPAN * tok_dev
    scale_factor = HEAD_DIM ** (-0.5)
    normed = layer_norm(tokens.astype(jnp.float32), ln_gain, ln_bias).astype(jnp.bfloat16)
    query = (jnp.dot(normed, w_qkv[0], preferred_element_type=jnp.float32) + b_qkv[0]).astype(
        jnp.bfloat16
    )
    key_value = (
        jnp.einsum("tc,kcd->tkd", normed, w_qkv[1:], preferred_element_type=jnp.float32) + b_qkv[1:]
    ).astype(jnp.bfloat16).reshape(tok_dev, 2 * local_width)
    group_rows = tok_dev // 4
    reach_groups = SPAN * group_rows
    padding = jnp.full((reach_groups,), -1, jnp.int32)
    padded_segment = jnp.concatenate([padding, segments, padding])

    window_segment = lax.optimization_barrier(
        jnp.repeat(
            lax.dynamic_slice_in_dim(padded_segment, seq_index * group_rows, (2 * SPAN + 1) * group_rows), 4
        )
    )

    def segment_window(key_start, length):
        return lax.dynamic_slice_in_dim(window_segment, key_start - row_start + reach_rows, length)

    query_segment = segment_window(row_start, tok_dev)
    query_heads = query.reshape(tok_dev, local_heads, HEAD_DIM)

    def block_scores(block, key_segment):
        key_heads = block[:, :local_width].reshape(-1, local_heads, HEAD_DIM)
        value_heads = block[:, local_width:].reshape(-1, local_heads, HEAD_DIM)
        scores = (
            jnp.einsum("qhd,khd->hqk", query_heads, key_heads, preferred_element_type=jnp.float32)
            * scale_factor
        )
        allowed = query_segment[:, None] == key_segment[None, :]
        return (jnp.where(allowed[None], scores, masked_score), value_heads)

    def absorb(state, blocks):
        row_top, totals, summed = state
        parts = [block_scores(block, key_segment) for block, key_segment in blocks]
        new_top = row_top
        for scores, _ in parts:
            new_top = jnp.maximum(new_top, jnp.max(scores, axis=-1, keepdims=True))
        factor = jnp.exp(row_top - new_top)
        totals = totals * factor
        summed = summed * factor
        for scores, value_heads in parts:
            weights = jnp.exp(scores - new_top)
            totals = totals + jnp.sum(weights, axis=-1, keepdims=True)
            summed = summed + jnp.einsum(
                "hqk,khd->hqd",
                weights.astype(jnp.bfloat16),
                value_heads,
                preferred_element_type=jnp.float32,
            )
        return (new_top, totals, summed)

    start_state = (
        jnp.full((local_heads, tok_dev, 1), masked_score, jnp.float32),
        jnp.zeros((local_heads, tok_dev, 1), jnp.float32),
        jnp.zeros((local_heads, tok_dev, HEAD_DIM), jnp.float32),
    )
    sign = 1 - 2 * (seq_index % 2)

    def swap(value):
        return lax.ppermute(value, "seq", [(i, i ^ 1) for i in range(seq_count)])

    def at(block, offset):
        return (block, segment_window(row_start + offset * tok_dev, tok_dev))

    below_4 = from_behind(key_value, "seq", 4)
    above_4 = from_behind(key_value, "seq", -4)
    below_2 = from_behind(key_value, "seq", 2)
    above_2 = from_behind(key_value, "seq", -2)
    partner_own = swap(key_value)
    partner_near = swap(jnp.concatenate([below_2, above_2], axis=0))
    partner_far = swap(jnp.where(sign > 0, above_4, below_4))
    state = absorb(start_state, [(key_value, query_segment), at(partner_own, sign)])
    state = absorb(
        state,
        [
            at(below_2, -2),
            at(above_2, 2),
            at(partner_near[:tok_dev], sign - 2),
            at(partner_near[tok_dev:], sign + 2),
        ],
    )
    state = absorb(state, [at(below_4, -4), at(above_4, 4), at(partner_far, -3 * sign)])
    row_top, totals, summed = state
    tp_index = lax.axis_index("tp")
    quarter = tok_dev // 4
    by_token = (summed / totals).reshape(local_heads, quarter, 4, HEAD_DIM)
    attended = jnp.transpose(by_token, (2, 1, 0, 3)).reshape(4, quarter, local_width).astype(jnp.bfloat16)
    head_term = jnp.einsum(
        "tgc,cd->tgd", attended, w_out, preferred_element_type=jnp.float32
    ).astype(jnp.bfloat16)
    head_terms = lax.all_to_all(head_term, "tp", split_axis=0, concat_axis=0, tiled=True)
    head_total = jnp.sum(head_terms.astype(jnp.float32), axis=0)
    own_tokens = lax.dynamic_index_in_dim(
        tokens.reshape(quarter, 4, model_width), tp_index, 1, keepdims=False
    )
    own_rows = own_tokens.astype(jnp.float32) + head_total + b_out
    merged_rows = layer_norm(own_rows, merge_gain, merge_bias).astype(jnp.bfloat16)
    owner_rows = owners[:, 0]
    capacity = max(2, 2 * quarter // seq_count)
    owner_table = (owner_rows[:, None] == jnp.arange(seq_count, dtype=jnp.int32)[None, :]).astype(
        jnp.int32
    )
    earlier = jnp.cumsum(owner_table, axis=0) - owner_table
    row_slot = jnp.sum(earlier * owner_table, axis=1)
    target_row = owner_rows * capacity + row_slot
    placing = (
        jnp.arange(seq_count * capacity, dtype=jnp.int32)[:, None] == target_row[None, :]
    ).astype(jnp.bfloat16)
    outgoing = jnp.dot(placing, merged_rows, preferred_element_type=jnp.float32).astype(
        jnp.bfloat16
    )
    return lax.all_to_all(outgoing, "seq", split_axis=0, concat_axis=0, tiled=True)


def solution(mesh):
    placed = (
        P("seq", None),
        P(),
        P(),
        P(None, None, "tp"),
        P(None, "tp"),
        P("tp", None),
        P(),
        P(),
        P(),
        P(),
        P("seq", None),
    )
    return jax.shard_map(
        per_device, mesh=mesh, in_specs=placed, out_specs=P("seq", "tp"), check_vma=False
    )
```

```python
import jax
import jax.numpy as jnp
from jax import lax
from jax.sharding import PartitionSpec as P

HEAD_DIM = 80
SPAN = 4


epsilon = 1e-06
masked_score = -1e30


def from_behind(value, axis, steps):
    count = lax.axis_size(axis)
    leading, last = (max(0, -steps), min(count, count - steps))
    return lax.ppermute(value, axis, [(source, source + steps) for source in range(leading, last)])


def layer_norm(values, gain_row, shift_row):
    center = jnp.mean(values, axis=-1, keepdims=True)
    centered = values - center
    spread = jnp.mean(centered * centered, axis=-1, keepdims=True)
    return centered * lax.rsqrt(spread + epsilon) * gain_row + shift_row


def per_device(
    tokens, ln_gain, ln_bias, w_qkv, b_qkv, w_out, b_out, merge_gain, merge_bias, segments, owners
):
    tok_dev = tokens.shape[0]
    model_width = tokens.shape[1]
    local_width = w_qkv.shape[2]
    local_heads = local_width // HEAD_DIM
    seq_count = lax.axis_size("seq")
    seq_index = lax.axis_index("seq")
    row_start = seq_index * tok_dev
    reach_rows = SPAN * tok_dev
    scale_factor = HEAD_DIM ** (-0.5)
    normed = layer_norm(tokens.astype(jnp.float32), ln_gain, ln_bias).astype(jnp.bfloat16)
    core = seq_index % 2
    pair_heads = local_heads // 2
    pair_width = pair_heads * HEAD_DIM
    chip_rows = 2 * tok_dev
    chip_start = (seq_index - core) * tok_dev
    reach_chips = SPAN // 2

    def swap(value):
        return lax.ppermute(value, "seq", [(i, i ^ 1) for i in range(seq_count)])

    def by_core(first, second):
        return jnp.where(core == 0, first, second)

    qkv = (
        jnp.einsum("tc,kcd->tkd", normed, w_qkv, preferred_element_type=jnp.float32) + b_qkv
    ).astype(jnp.bfloat16).reshape(tok_dev, 3, 2, pair_width)
    mine = lax.dynamic_index_in_dim(qkv, core, 2, keepdims=False)
    other = lax.dynamic_index_in_dim(qkv, 1 - core, 2, keepdims=False)
    received = swap(other)
    chip_qkv = jnp.concatenate([by_core(mine, received), by_core(received, mine)], axis=0)
    query_heads = chip_qkv[:, 0].reshape(chip_rows, pair_heads, HEAD_DIM)
    chip_kv = chip_qkv[:, 1:]

    group_rows = tok_dev // 4
    reach_groups = SPAN * group_rows
    padding = jnp.full((reach_groups,), -1, jnp.int32)
    padded_segment = jnp.concatenate([padding, segments, padding])
    window_segment = lax.optimization_barrier(
        jnp.repeat(
            lax.dynamic_slice_in_dim(
                padded_segment, chip_start // 4, (2 * reach_chips + 1) * chip_rows // 4
            ),
            4,
        )
    )

    def segment_window(offset):
        return lax.dynamic_slice_in_dim(window_segment, (offset + reach_chips) * chip_rows, chip_rows)

    query_segment = segment_window(0)

    def absorb(state, block, offset):
        row_top, totals, summed = state
        key_heads = block[:, 0].reshape(-1, pair_heads, HEAD_DIM)
        value_heads = block[:, 1].reshape(-1, pair_heads, HEAD_DIM)
        scores = (
            jnp.einsum("qhd,khd->hqk", query_heads, key_heads, preferred_element_type=jnp.float32)
            * scale_factor
        )
        allowed = query_segment[:, None] == segment_window(offset)[None, :]
        scores = jnp.where(allowed[None], scores, masked_score)
        new_top = jnp.maximum(row_top, jnp.max(scores, axis=-1, keepdims=True))
        factor = jnp.exp(row_top - new_top)
        weights = jnp.exp(scores - new_top)
        totals = totals * factor + jnp.sum(weights, axis=-1, keepdims=True)
        summed = summed * factor + jnp.einsum(
            "hqk,khd->hqd",
            weights.astype(jnp.bfloat16),
            value_heads,
            preferred_element_type=jnp.float32,
        )
        return (new_top, totals, summed)

    start_state = (
        jnp.full((pair_heads, chip_rows, 1), masked_score, jnp.float32),
        jnp.zeros((pair_heads, chip_rows, 1), jnp.float32),
        jnp.zeros((pair_heads, chip_rows, HEAD_DIM), jnp.float32),
    )
    below_1 = from_behind(chip_kv, "seq", 2)
    above_1 = from_behind(chip_kv, "seq", -2)
    below_2 = from_behind(chip_kv, "seq", 4)
    above_2 = from_behind(chip_kv, "seq", -4)
    state = absorb(start_state, chip_kv, 0)
    state = absorb(state, below_1, -1)
    state = absorb(state, above_1, 1)
    state = absorb(state, below_2, -2)
    state = absorb(state, above_2, 2)
    row_top, totals, summed = state
    pair_out = jnp.transpose(summed / totals, (1, 0, 2)).reshape(chip_rows, pair_width).astype(jnp.bfloat16)
    own_part = by_core(pair_out[:tok_dev], pair_out[tok_dev:])
    other_part = swap(by_core(pair_out[tok_dev:], pair_out[:tok_dev]))
    attended_rows = jnp.concatenate([by_core(own_part, other_part), by_core(other_part, own_part)], axis=1)
    tp_index = lax.axis_index("tp")
    quarter = tok_dev // 4
    attended = jnp.transpose(attended_rows.reshape(quarter, 4, local_width), (1, 0, 2))
    head_term = jnp.einsum(
        "tgc,cd->tgd", attended, w_out, preferred_element_type=jnp.float32
    ).astype(jnp.bfloat16)
    head_terms = lax.all_to_all(head_term, "tp", split_axis=0, concat_axis=0, tiled=True)
    head_total = jnp.sum(head_terms.astype(jnp.float32), axis=0)
    own_tokens = lax.dynamic_index_in_dim(
        tokens.reshape(quarter, 4, model_width), tp_index, 1, keepdims=False
    )
    own_rows = own_tokens.astype(jnp.float32) + head_total + b_out
    merged_rows = layer_norm(own_rows, merge_gain, merge_bias).astype(jnp.bfloat16)
    owner_rows = owners[:, 0]
    capacity = max(2, 2 * quarter // seq_count)
    owner_table = (owner_rows[:, None] == jnp.arange(seq_count, dtype=jnp.int32)[None, :]).astype(
        jnp.int32
    )
    earlier = jnp.cumsum(owner_table, axis=0) - owner_table
    row_slot = jnp.sum(earlier * owner_table, axis=1)
    target_row = owner_rows * capacity + row_slot
    placing = (
        jnp.arange(seq_count * capacity, dtype=jnp.int32)[:, None] == target_row[None, :]
    ).astype(jnp.bfloat16)
    outgoing = jnp.dot(placing, merged_rows, preferred_element_type=jnp.float32).astype(
        jnp.bfloat16
    )
    return lax.all_to_all(outgoing, "seq", split_axis=0, concat_axis=0, tiled=True)


def solution(mesh):
    placed = (
        P("seq", None),
        P(),
        P(),
        P(None, None, "tp"),
        P(None, "tp"),
        P("tp", None),
        P(),
        P(),
        P(),
        P(),
        P("seq", None),
    )
    return jax.shard_map(
        per_device, mesh=mesh, in_specs=placed, out_specs=P("seq", "tp"), check_vma=False
    )
```

```python
import jax
import jax.numpy as jnp
from jax import lax
from jax.sharding import PartitionSpec as P

HEAD_DIM = 80
SPAN = 4


epsilon = 1e-06
masked_score = -1e30


def from_behind(value, axis, steps):
    count = lax.axis_size(axis)
    leading, last = (max(0, -steps), min(count, count - steps))
    return lax.ppermute(value, axis, [(source, source + steps) for source in range(leading, last)])


def layer_norm(values, gain_row, shift_row):
    center = jnp.mean(values, axis=-1, keepdims=True)
    centered = values - center
    spread = jnp.mean(centered * centered, axis=-1, keepdims=True)
    return centered * lax.rsqrt(spread + epsilon) * gain_row + shift_row


def per_device(
    tokens, ln_gain, ln_bias, w_qkv, b_qkv, w_out, b_out, merge_gain, merge_bias, segments, owners
):
    tok_dev = tokens.shape[0]
    model_width = tokens.shape[1]
    local_width = w_qkv.shape[2]
    local_heads = local_width // HEAD_DIM
    seq_count = lax.axis_size("seq")
    seq_index = lax.axis_index("seq")
    row_start = seq_index * tok_dev
    reach_rows = SPAN * tok_dev
    scale_factor = HEAD_DIM ** (-0.5)
    normed = layer_norm(tokens.astype(jnp.float32), ln_gain, ln_bias).astype(jnp.bfloat16)
    query = (jnp.dot(normed, w_qkv[0], preferred_element_type=jnp.float32) + b_qkv[0]).astype(
        jnp.bfloat16
    )
    key_value = (
        jnp.einsum("tc,kcd->ktd", normed, w_qkv[1:], preferred_element_type=jnp.float32)
        + b_qkv[1:, None, :]
    ).astype(jnp.bfloat16)
    group_rows = tok_dev // 4
    reach_groups = SPAN * group_rows
    padding = jnp.full((reach_groups,), -1, jnp.int32)
    padded_segment = jnp.concatenate([padding, segments, padding])

    window_segment = lax.optimization_barrier(
        jnp.repeat(
            lax.dynamic_slice_in_dim(padded_segment, seq_index * group_rows, (2 * SPAN + 1) * group_rows), 4
        )
    )

    def segment_window(key_start, length):
        return lax.dynamic_slice_in_dim(window_segment, key_start - row_start + reach_rows, length)

    query_segment = segment_window(row_start, tok_dev)
    query_heads = query.reshape(tok_dev, local_heads, HEAD_DIM)

    def block_scores(block, key_segment):
        key_heads = block[0].reshape(-1, local_heads, HEAD_DIM)
        value_heads = block[1].reshape(-1, local_heads, HEAD_DIM)
        scores = (
            jnp.einsum("qhd,khd->hqk", query_heads, key_heads, preferred_element_type=jnp.float32)
            * scale_factor
        )
        allowed = query_segment[:, None] == key_segment[None, :]
        return (jnp.where(allowed[None], scores, masked_score), value_heads)

    def absorb(state, block, key_segment):
        row_top, totals, summed = state
        scores, value_heads = block_scores(block, key_segment)
        new_top = jnp.maximum(row_top, jnp.max(scores, axis=-1, keepdims=True))
        factor = jnp.exp(row_top - new_top)
        weights = jnp.exp(scores - new_top)
        totals = totals * factor + jnp.sum(weights, axis=-1, keepdims=True)
        summed = summed * factor + jnp.einsum(
            "hqk,khd->hqd",
            weights.astype(jnp.bfloat16),
            value_heads,
            preferred_element_type=jnp.float32,
        )
        return (new_top, totals, summed)

    def absorb_remote(state, block, key_start):
        key_segment = segment_window(key_start, tok_dev)
        return absorb(state, block, key_segment)

    start_state = (
        jnp.full((local_heads, tok_dev, 1), masked_score, jnp.float32),
        jnp.zeros((local_heads, tok_dev, 1), jnp.float32),
        jnp.zeros((local_heads, tok_dev, HEAD_DIM), jnp.float32),
    )
    sign = 1 - 2 * (seq_index % 2)

    def swap(value):
        return lax.ppermute(value, "seq", [(i, i ^ 1) for i in range(seq_count)])

    def absorb_at(state, block, offset):
        return absorb_remote(state, block, row_start + offset * tok_dev)

    below_2 = from_behind(key_value, "seq", 2)
    above_2 = from_behind(key_value, "seq", -2)
    below_4 = from_behind(key_value, "seq", 4)
    above_4 = from_behind(key_value, "seq", -4)
    partner_own = swap(key_value)
    state = absorb(start_state, key_value, query_segment)
    partner_near = swap(jnp.concatenate([below_2, above_2], axis=0))
    partner_far = swap(jnp.where(sign > 0, above_4, below_4))
    state = absorb_at(state, partner_own, sign)
    state = absorb_at(state, below_2, -2)
    state = absorb_at(state, above_2, 2)
    state = absorb_at(state, partner_near[:2], sign - 2)
    state = absorb_at(state, partner_near[2:], sign + 2)
    state = absorb_at(state, below_4, -4)
    state = absorb_at(state, above_4, 4)
    state = absorb_at(state, partner_far, -3 * sign)
    row_top, totals, summed = state
    tp_index = lax.axis_index("tp")
    quarter = tok_dev // 4
    by_token = (summed / totals).reshape(local_heads, quarter, 4, HEAD_DIM)
    attended = jnp.transpose(by_token, (2, 1, 0, 3)).reshape(4, quarter, local_width).astype(jnp.bfloat16)
    head_term = jnp.einsum(
        "tgc,cd->tgd", attended, w_out, preferred_element_type=jnp.float32
    ).astype(jnp.bfloat16)
    head_terms = lax.all_to_all(head_term, "tp", split_axis=0, concat_axis=0, tiled=True)
    head_total = jnp.sum(head_terms.astype(jnp.float32), axis=0)
    own_tokens = lax.dynamic_index_in_dim(
        tokens.reshape(quarter, 4, model_width), tp_index, 1, keepdims=False
    )
    own_rows = own_tokens.astype(jnp.float32) + head_total + b_out
    merged_rows = layer_norm(own_rows, merge_gain, merge_bias).astype(jnp.bfloat16)
    owner_rows = owners[:, 0]
    capacity = max(2, 2 * quarter // seq_count)
    owner_table = (owner_rows[:, None] == jnp.arange(seq_count, dtype=jnp.int32)[None, :]).astype(
        jnp.int32
    )
    earlier = jnp.cumsum(owner_table, axis=0) - owner_table
    row_slot = jnp.sum(earlier * owner_table, axis=1)
    target_row = owner_rows * capacity + row_slot
    placing = (
        jnp.arange(seq_count * capacity, dtype=jnp.int32)[:, None] == target_row[None, :]
    ).astype(jnp.bfloat16)
    outgoing = jnp.dot(placing, merged_rows, preferred_element_type=jnp.float32).astype(
        jnp.bfloat16
    )
    return lax.all_to_all(outgoing, "seq", split_axis=0, concat_axis=0, tiled=True)


def solution(mesh):
    placed = (
        P("seq", None),
        P(),
        P(),
        P(None, None, "tp"),
        P(None, "tp"),
        P("tp", None),
        P(),
        P(),
        P(),
        P(),
        P("seq", None),
    )
    return jax.shard_map(
        per_device, mesh=mesh, in_specs=placed, out_specs=P("seq", "tp"), check_vma=False
    )
```

```python
import jax
import jax.numpy as jnp
from jax import lax
from jax.sharding import PartitionSpec as P

HEAD_DIM = 80
SPAN = 4


epsilon = 1e-06
masked_score = -1e30


def from_behind(value, axis, steps):
    count = lax.axis_size(axis)
    leading, last = (max(0, -steps), min(count, count - steps))
    return lax.ppermute(value, axis, [(source, source + steps) for source in range(leading, last)])


def layer_norm(values, gain_row, shift_row):
    center = jnp.mean(values, axis=-1, keepdims=True)
    centered = values - center
    spread = jnp.mean(centered * centered, axis=-1, keepdims=True)
    return centered * lax.rsqrt(spread + epsilon) * gain_row + shift_row


def per_device(
    tokens, ln_gain, ln_bias, w_qkv, b_qkv, w_out, b_out, merge_gain, merge_bias, segments, owners
):
    tok_dev = tokens.shape[0]
    model_width = tokens.shape[1]
    local_width = w_qkv.shape[2]
    local_heads = local_width // HEAD_DIM
    seq_count = lax.axis_size("seq")
    seq_index = lax.axis_index("seq")
    row_start = seq_index * tok_dev
    reach_rows = SPAN * tok_dev
    scale_factor = HEAD_DIM ** (-0.5)
    normed = layer_norm(tokens.astype(jnp.float32), ln_gain, ln_bias).astype(jnp.bfloat16)
    query = (jnp.dot(normed, w_qkv[0], preferred_element_type=jnp.float32) + b_qkv[0]).astype(
        jnp.bfloat16
    )
    key_value = (
        jnp.einsum("tc,kcd->ktd", normed, w_qkv[1:], preferred_element_type=jnp.float32)
        + b_qkv[1:, None, :]
    ).astype(jnp.bfloat16)
    group_rows = tok_dev // 4
    reach_groups = SPAN * group_rows
    padding = jnp.full((reach_groups,), -1, jnp.int32)
    padded_segment = jnp.concatenate([padding, segments, padding])

    window_segment = lax.optimization_barrier(
        jnp.repeat(
            lax.dynamic_slice_in_dim(padded_segment, seq_index * group_rows, (2 * SPAN + 1) * group_rows), 4
        )
    )

    def segment_window(key_start, length):
        return lax.dynamic_slice_in_dim(window_segment, key_start - row_start + reach_rows, length)

    query_segment = segment_window(row_start, tok_dev)
    query_heads = query.reshape(tok_dev, local_heads, HEAD_DIM)

    def block_scores(block, key_segment):
        key_heads = block[0].reshape(-1, local_heads, HEAD_DIM)
        value_heads = block[1].reshape(-1, local_heads, HEAD_DIM)
        scores = (
            jnp.einsum("qhd,khd->hqk", query_heads, key_heads, preferred_element_type=jnp.float32)
            * scale_factor
        )
        allowed = query_segment[:, None] == key_segment[None, :]
        return (jnp.where(allowed[None], scores, masked_score), value_heads)

    def absorb(state, block, key_segment):
        row_top, totals, summed = state
        scores, value_heads = block_scores(block, key_segment)
        new_top = jnp.maximum(row_top, jnp.max(scores, axis=-1, keepdims=True))
        factor = jnp.exp(row_top - new_top)
        weights = jnp.exp(scores - new_top)
        totals = totals * factor + jnp.sum(weights, axis=-1, keepdims=True)
        summed = summed * factor + jnp.einsum(
            "hqk,khd->hqd",
            weights.astype(jnp.bfloat16),
            value_heads,
            preferred_element_type=jnp.float32,
        )
        return (new_top, totals, summed)

    def absorb_remote(state, block, key_start):
        key_segment = segment_window(key_start, tok_dev)
        return absorb(state, block, key_segment)

    start_state = (
        jnp.full((local_heads, tok_dev, 1), masked_score, jnp.float32),
        jnp.zeros((local_heads, tok_dev, 1), jnp.float32),
        jnp.zeros((local_heads, tok_dev, HEAD_DIM), jnp.float32),
    )
    sign = 1 - 2 * (seq_index % 2)

    def swap(value):
        return lax.ppermute(value, "seq", [(i, i ^ 1) for i in range(seq_count)])

    def absorb_at(state, block, offset):
        return absorb_remote(state, block, row_start + offset * tok_dev)

    below_2 = from_behind(key_value, "seq", 2)
    above_2 = from_behind(key_value, "seq", -2)
    below_4 = from_behind(key_value, "seq", 4)
    above_4 = from_behind(key_value, "seq", -4)
    state = absorb(start_state, key_value, query_segment)
    partner_near = swap(jnp.concatenate([key_value, below_2, above_2], axis=0))
    partner_far = swap(jnp.where(sign > 0, above_4, below_4))
    state = absorb_at(state, below_2, -2)
    state = absorb_at(state, above_2, 2)
    state = absorb_at(state, partner_near[:2], sign)
    state = absorb_at(state, partner_near[2:4], sign - 2)
    state = absorb_at(state, partner_near[4:], sign + 2)
    state = absorb_at(state, below_4, -4)
    state = absorb_at(state, above_4, 4)
    state = absorb_at(state, partner_far, -3 * sign)
    row_top, totals, summed = state
    tp_index = lax.axis_index("tp")
    quarter = tok_dev // 4
    by_token = (summed / totals).reshape(local_heads, quarter, 4, HEAD_DIM)
    attended = jnp.transpose(by_token, (2, 1, 0, 3)).reshape(4, quarter, local_width).astype(jnp.bfloat16)
    head_term = jnp.einsum(
        "tgc,cd->tgd", attended, w_out, preferred_element_type=jnp.float32
    ).astype(jnp.bfloat16)
    head_terms = lax.all_to_all(head_term, "tp", split_axis=0, concat_axis=0, tiled=True)
    head_total = jnp.sum(head_terms.astype(jnp.float32), axis=0)
    own_tokens = lax.dynamic_index_in_dim(
        tokens.reshape(quarter, 4, model_width), tp_index, 1, keepdims=False
    )
    own_rows = own_tokens.astype(jnp.float32) + head_total + b_out
    merged_rows = layer_norm(own_rows, merge_gain, merge_bias).astype(jnp.bfloat16)
    owner_rows = owners[:, 0]
    capacity = max(2, 2 * quarter // seq_count)
    owner_table = (owner_rows[:, None] == jnp.arange(seq_count, dtype=jnp.int32)[None, :]).astype(
        jnp.int32
    )
    earlier = jnp.cumsum(owner_table, axis=0) - owner_table
    row_slot = jnp.sum(earlier * owner_table, axis=1)
    target_row = owner_rows * capacity + row_slot
    placing = (
        jnp.arange(seq_count * capacity, dtype=jnp.int32)[:, None] == target_row[None, :]
    ).astype(jnp.bfloat16)
    outgoing = jnp.dot(placing, merged_rows, preferred_element_type=jnp.float32).astype(
        jnp.bfloat16
    )
    return lax.all_to_all(outgoing, "seq", split_axis=0, concat_axis=0, tiled=True)


def solution(mesh):
    placed = (
        P("seq", None),
        P(),
        P(),
        P(None, None, "tp"),
        P(None, "tp"),
        P("tp", None),
        P(),
        P(),
        P(),
        P(),
        P("seq", None),
    )
    return jax.shard_map(
        per_device, mesh=mesh, in_specs=placed, out_specs=P("seq", "tp"), check_vma=False
    )
```

```python
import jax
import jax.numpy as jnp
from jax import lax
from jax.sharding import PartitionSpec as P

HEAD_DIM = 80
SPAN = 4


epsilon = 1e-06
masked_score = -1e30


def from_behind(value, axis, steps):
    count = lax.axis_size(axis)
    leading, last = (max(0, -steps), min(count, count - steps))
    return lax.ppermute(value, axis, [(source, source + steps) for source in range(leading, last)])


def layer_norm(values, gain_row, shift_row):
    center = jnp.mean(values, axis=-1, keepdims=True)
    centered = values - center
    spread = jnp.mean(centered * centered, axis=-1, keepdims=True)
    return centered * lax.rsqrt(spread + epsilon) * gain_row + shift_row


def per_device(
    tokens, ln_gain, ln_bias, w_qkv, b_qkv, w_out, b_out, merge_gain, merge_bias, segments, owners
):
    tok_dev = tokens.shape[0]
    model_width = tokens.shape[1]
    local_width = w_qkv.shape[2]
    local_heads = local_width // HEAD_DIM
    seq_count = lax.axis_size("seq")
    seq_index = lax.axis_index("seq")
    row_start = seq_index * tok_dev
    reach_rows = SPAN * tok_dev
    scale_factor = HEAD_DIM ** (-0.5)
    ones = jnp.ones((model_width, 1), jnp.float32)
    center = jnp.dot(tokens, ones.astype(tokens.dtype), preferred_element_type=jnp.float32) / model_width
    centered = tokens.astype(jnp.float32) - center
    spread = (
        jnp.dot(centered * centered, ones, precision=lax.Precision.HIGHEST, preferred_element_type=jnp.float32)
        / model_width
    )
    normed = (centered * lax.rsqrt(spread + epsilon) * ln_gain + ln_bias).astype(jnp.bfloat16)
    query = (jnp.dot(normed, w_qkv[0], preferred_element_type=jnp.float32) + b_qkv[0]).astype(
        jnp.bfloat16
    )
    key_value = (
        jnp.einsum("tc,kcd->ktd", normed, w_qkv[1:], preferred_element_type=jnp.float32)
        + b_qkv[1:, None, :]
    ).astype(jnp.bfloat16)
    group_rows = tok_dev // 4
    reach_groups = SPAN * group_rows
    padding = jnp.full((reach_groups,), -1, jnp.int32)
    padded_segment = jnp.concatenate([padding, segments, padding])

    window_segment = lax.optimization_barrier(
        jnp.repeat(
            lax.dynamic_slice_in_dim(padded_segment, seq_index * group_rows, (2 * SPAN + 1) * group_rows), 4
        )
    )

    def segment_window(key_start, length):
        return lax.dynamic_slice_in_dim(window_segment, key_start - row_start + reach_rows, length)

    query_segment = segment_window(row_start, tok_dev)
    query_heads = query.reshape(tok_dev, local_heads, HEAD_DIM)

    def block_scores(block, key_segment):
        key_heads = block[0].reshape(-1, local_heads, HEAD_DIM)
        value_heads = block[1].reshape(-1, local_heads, HEAD_DIM)
        scores = (
            jnp.einsum("qhd,khd->hqk", query_heads, key_heads, preferred_element_type=jnp.float32)
            * scale_factor
        )
        allowed = query_segment[:, None] == key_segment[None, :]
        return (jnp.where(allowed[None], scores, masked_score), value_heads)

    def absorb(state, block, key_segment):
        row_top, totals, summed = state
        scores, value_heads = block_scores(block, key_segment)
        new_top = jnp.maximum(row_top, jnp.max(scores, axis=-1, keepdims=True))
        factor = jnp.exp(row_top - new_top)
        weights = jnp.exp(scores - new_top)
        totals = totals * factor + jnp.sum(weights, axis=-1, keepdims=True)
        summed = summed * factor + jnp.einsum(
            "hqk,khd->hqd",
            weights.astype(jnp.bfloat16),
            value_heads,
            preferred_element_type=jnp.float32,
        )
        return (new_top, totals, summed)

    def absorb_remote(state, block, key_start):
        key_segment = segment_window(key_start, tok_dev)
        return absorb(state, block, key_segment)

    start_state = (
        jnp.full((local_heads, tok_dev, 1), masked_score, jnp.float32),
        jnp.zeros((local_heads, tok_dev, 1), jnp.float32),
        jnp.zeros((local_heads, tok_dev, HEAD_DIM), jnp.float32),
    )
    sign = 1 - 2 * (seq_index % 2)

    def swap(value):
        return lax.ppermute(value, "seq", [(i, i ^ 1) for i in range(seq_count)])

    def absorb_at(state, block, offset):
        return absorb_remote(state, block, row_start + offset * tok_dev)

    below_2 = from_behind(key_value, "seq", 2)
    above_2 = from_behind(key_value, "seq", -2)
    below_4 = from_behind(key_value, "seq", 4)
    above_4 = from_behind(key_value, "seq", -4)
    partner_own = swap(key_value)
    state = absorb(start_state, key_value, query_segment)
    partner_near = swap(jnp.concatenate([below_2, above_2], axis=0))
    partner_far = swap(jnp.where(sign > 0, above_4, below_4))
    state = absorb_at(state, partner_own, sign)
    state = absorb_at(state, below_2, -2)
    state = absorb_at(state, above_2, 2)
    state = absorb_at(state, partner_near[:2], sign - 2)
    state = absorb_at(state, partner_near[2:], sign + 2)
    state = absorb_at(state, below_4, -4)
    state = absorb_at(state, above_4, 4)
    state = absorb_at(state, partner_far, -3 * sign)
    row_top, totals, summed = state
    tp_index = lax.axis_index("tp")
    quarter = tok_dev // 4
    by_token = (summed / totals).reshape(local_heads, quarter, 4, HEAD_DIM)
    attended = jnp.transpose(by_token, (2, 1, 0, 3)).reshape(4, quarter, local_width).astype(jnp.bfloat16)
    head_term = jnp.einsum(
        "tgc,cd->tgd", attended, w_out, preferred_element_type=jnp.float32
    ).astype(jnp.bfloat16)
    head_terms = lax.all_to_all(head_term, "tp", split_axis=0, concat_axis=0, tiled=True)
    head_total = jnp.sum(head_terms.astype(jnp.float32), axis=0)
    own_tokens = lax.dynamic_index_in_dim(
        tokens.reshape(quarter, 4, model_width), tp_index, 1, keepdims=False
    )
    own_rows = own_tokens.astype(jnp.float32) + head_total + b_out
    merged_rows = layer_norm(own_rows, merge_gain, merge_bias).astype(jnp.bfloat16)
    owner_rows = owners[:, 0]
    capacity = max(2, 2 * quarter // seq_count)
    owner_table = (owner_rows[:, None] == jnp.arange(seq_count, dtype=jnp.int32)[None, :]).astype(
        jnp.int32
    )
    earlier = jnp.cumsum(owner_table, axis=0) - owner_table
    row_slot = jnp.sum(earlier * owner_table, axis=1)
    target_row = owner_rows * capacity + row_slot
    placing = (
        jnp.arange(seq_count * capacity, dtype=jnp.int32)[:, None] == target_row[None, :]
    ).astype(jnp.bfloat16)
    outgoing = jnp.dot(placing, merged_rows, preferred_element_type=jnp.float32).astype(
        jnp.bfloat16
    )
    return lax.all_to_all(outgoing, "seq", split_axis=0, concat_axis=0, tiled=True)


def solution(mesh):
    placed = (
        P("seq", None),
        P(),
        P(),
        P(None, None, "tp"),
        P(None, "tp"),
        P("tp", None),
        P(),
        P(),
        P(),
        P(),
        P("seq", None),
    )
    return jax.shard_map(
        per_device, mesh=mesh, in_specs=placed, out_specs=P("seq", "tp"), check_vma=False
    )
```

```python
import jax
import jax.numpy as jnp
from jax import lax
from jax.sharding import PartitionSpec as P

HEAD_DIM = 80
SPAN = 4


epsilon = 1e-06
masked_score = -1e30


def from_behind(value, axis, steps):
    count = lax.axis_size(axis)
    leading, last = (max(0, -steps), min(count, count - steps))
    return lax.ppermute(value, axis, [(source, source + steps) for source in range(leading, last)])


def layer_norm(values, gain_row, shift_row):
    center = jnp.mean(values, axis=-1, keepdims=True)
    centered = values - center
    spread = jnp.mean(centered * centered, axis=-1, keepdims=True)
    return centered * lax.rsqrt(spread + epsilon) * gain_row + shift_row


def per_device(
    tokens, ln_gain, ln_bias, w_qkv, b_qkv, w_out, b_out, merge_gain, merge_bias, segments, owners
):
    tok_dev = tokens.shape[0]
    model_width = tokens.shape[1]
    local_width = w_qkv.shape[2]
    local_heads = local_width // HEAD_DIM
    seq_count = lax.axis_size("seq")
    seq_index = lax.axis_index("seq")
    row_start = seq_index * tok_dev
    reach_rows = SPAN * tok_dev
    scale_factor = HEAD_DIM ** (-0.5)
    normed = layer_norm(tokens.astype(jnp.float32), ln_gain, ln_bias).astype(jnp.bfloat16)
    query = (jnp.dot(normed, w_qkv[0], preferred_element_type=jnp.float32) + b_qkv[0]).astype(
        jnp.bfloat16
    )
    key_value = (
        jnp.einsum("tc,kcd->ktd", normed, w_qkv[1:], preferred_element_type=jnp.float32)
        + b_qkv[1:, None, :]
    ).astype(jnp.bfloat16)
    group_rows = tok_dev // 4
    reach_groups = SPAN * group_rows
    padding = jnp.full((reach_groups,), -1, jnp.int32)
    padded_segment = jnp.concatenate([padding, segments, padding])

    window_segment = lax.optimization_barrier(
        jnp.repeat(
            lax.dynamic_slice_in_dim(padded_segment, seq_index * group_rows, (2 * SPAN + 1) * group_rows), 4
        )
    )

    def segment_window(key_start, length):
        return lax.dynamic_slice_in_dim(window_segment, key_start - row_start + reach_rows, length)

    query_segment = segment_window(row_start, tok_dev)
    query_heads = query.reshape(tok_dev, local_heads, HEAD_DIM)

    def block_scores(block, key_segment):
        key_heads = block[0].reshape(-1, local_heads, HEAD_DIM)
        value_heads = block[1].reshape(-1, local_heads, HEAD_DIM)
        scores = (
            jnp.einsum("qhd,khd->hqk", query_heads, key_heads, preferred_element_type=jnp.float32)
            * scale_factor
        )
        allowed = query_segment[:, None] == key_segment[None, :]
        return (jnp.where(allowed[None], scores, masked_score), value_heads)

    def absorb(state, block, key_segment):
        row_top, totals, summed = state
        scores, value_heads = block_scores(block, key_segment)
        new_top = jnp.maximum(row_top, jnp.max(scores, axis=-1, keepdims=True))
        factor = jnp.exp(row_top - new_top)
        weights = jnp.exp(scores - new_top)
        totals = totals * factor + jnp.sum(weights, axis=-1, keepdims=True)
        summed = summed * factor + jnp.einsum(
            "hqk,khd->hqd",
            weights.astype(jnp.bfloat16),
            value_heads,
            preferred_element_type=jnp.float32,
        )
        return (new_top, totals, summed)

    def absorb_remote(state, block, key_start):
        key_segment = segment_window(key_start, tok_dev)
        return absorb(state, block, key_segment)

    start_state = (
        jnp.full((local_heads, tok_dev, 1), masked_score, jnp.float32),
        jnp.zeros((local_heads, tok_dev, 1), jnp.float32),
        jnp.zeros((local_heads, tok_dev, HEAD_DIM), jnp.float32),
    )
    sign = 1 - 2 * (seq_index % 2)

    def swap(value):
        return lax.ppermute(value, "seq", [(i, i ^ 1) for i in range(seq_count)])

    def absorb_at(state, block, offset):
        return absorb_remote(state, block, row_start + offset * tok_dev)

    below_2 = from_behind(key_value, "seq", 2)
    above_2 = from_behind(key_value, "seq", -2)
    below_4 = from_behind(key_value, "seq", 4)
    above_4 = from_behind(key_value, "seq", -4)
    partner_own = swap(key_value)
    state = absorb(start_state, key_value, query_segment)
    partner_near = swap(jnp.concatenate([below_2, above_2], axis=0))
    partner_below = swap(below_4)
    partner_above = swap(above_4)
    state = absorb_at(state, partner_own, sign)
    state = absorb_at(state, below_2, -2)
    state = absorb_at(state, above_2, 2)
    state = absorb_at(state, partner_near[:2], sign - 2)
    state = absorb_at(state, partner_near[2:], sign + 2)
    state = absorb_at(state, below_4, -4)
    state = absorb_at(state, above_4, 4)
    state = absorb_at(state, jnp.where(sign > 0, partner_below, partner_above), -3 * sign)
    row_top, totals, summed = state
    tp_index = lax.axis_index("tp")
    quarter = tok_dev // 4
    by_token = (summed / totals).reshape(local_heads, quarter, 4, HEAD_DIM)
    attended = jnp.transpose(by_token, (2, 1, 0, 3)).reshape(4, quarter, local_width).astype(jnp.bfloat16)
    head_term = jnp.einsum(
        "tgc,cd->tgd", attended, w_out, preferred_element_type=jnp.float32
    ).astype(jnp.bfloat16)
    head_terms = lax.all_to_all(head_term, "tp", split_axis=0, concat_axis=0, tiled=True)
    head_total = jnp.sum(head_terms.astype(jnp.float32), axis=0)
    own_tokens = lax.dynamic_index_in_dim(
        tokens.reshape(quarter, 4, model_width), tp_index, 1, keepdims=False
    )
    own_rows = own_tokens.astype(jnp.float32) + head_total + b_out
    merged_rows = layer_norm(own_rows, merge_gain, merge_bias).astype(jnp.bfloat16)
    owner_rows = owners[:, 0]
    capacity = max(2, 2 * quarter // seq_count)
    owner_table = (owner_rows[:, None] == jnp.arange(seq_count, dtype=jnp.int32)[None, :]).astype(
        jnp.int32
    )
    earlier = jnp.cumsum(owner_table, axis=0) - owner_table
    row_slot = jnp.sum(earlier * owner_table, axis=1)
    target_row = owner_rows * capacity + row_slot
    placing = (
        jnp.arange(seq_count * capacity, dtype=jnp.int32)[:, None] == target_row[None, :]
    ).astype(jnp.bfloat16)
    outgoing = jnp.dot(placing, merged_rows, preferred_element_type=jnp.float32).astype(
        jnp.bfloat16
    )
    return lax.all_to_all(outgoing, "seq", split_axis=0, concat_axis=0, tiled=True)


def solution(mesh):
    placed = (
        P("seq", None),
        P(),
        P(),
        P(None, None, "tp"),
        P(None, "tp"),
        P("tp", None),
        P(),
        P(),
        P(),
        P(),
        P("seq", None),
    )
    return jax.shard_map(
        per_device, mesh=mesh, in_specs=placed, out_specs=P("seq", "tp"), check_vma=False
    )
```

```python
import jax
import jax.numpy as jnp
from jax import lax
from jax.sharding import PartitionSpec as P

HEAD_DIM = 80
SPAN = 4


epsilon = 1e-06
masked_score = -1e30


def from_behind(value, axis, steps):
    count = lax.axis_size(axis)
    leading, last = (max(0, -steps), min(count, count - steps))
    return lax.ppermute(value, axis, [(source, source + steps) for source in range(leading, last)])


def layer_norm(values, gain_row, shift_row):
    center = jnp.mean(values, axis=-1, keepdims=True)
    centered = values - center
    spread = jnp.mean(centered * centered, axis=-1, keepdims=True)
    return centered * lax.rsqrt(spread + epsilon) * gain_row + shift_row


def per_device(
    tokens, ln_gain, ln_bias, w_qkv, b_qkv, w_out, b_out, merge_gain, merge_bias, segments, owners
):
    tok_dev = tokens.shape[0]
    model_width = tokens.shape[1]
    local_width = w_qkv.shape[2]
    local_heads = local_width // HEAD_DIM
    seq_count = lax.axis_size("seq")
    seq_index = lax.axis_index("seq")
    row_start = seq_index * tok_dev
    reach_rows = SPAN * tok_dev
    scale_factor = HEAD_DIM ** (-0.5)
    normed = layer_norm(tokens.astype(jnp.float32), ln_gain, ln_bias).astype(jnp.bfloat16)
    query = (jnp.dot(normed, w_qkv[0], preferred_element_type=jnp.float32) + b_qkv[0]).astype(
        jnp.bfloat16
    )
    key_value = (
        jnp.einsum("tc,kcd->ktd", normed, w_qkv[1:], preferred_element_type=jnp.float32)
        + b_qkv[1:, None, :]
    ).astype(jnp.bfloat16)
    group_rows = tok_dev // 4
    reach_groups = SPAN * group_rows
    padding = jnp.full((reach_groups,), -1, jnp.int32)
    padded_segment = jnp.concatenate([padding, segments, padding])

    window_segment = lax.optimization_barrier(
        jnp.repeat(
            lax.dynamic_slice_in_dim(padded_segment, seq_index * group_rows, (2 * SPAN + 1) * group_rows), 4
        )
    )

    def segment_window(key_start, length):
        return lax.dynamic_slice_in_dim(window_segment, key_start - row_start + reach_rows, length)

    query_segment = segment_window(row_start, tok_dev)
    query_heads = query.reshape(tok_dev, local_heads, HEAD_DIM)

    def block_scores(block, key_segment):
        key_heads = block[0].reshape(-1, local_heads, HEAD_DIM)
        value_heads = block[1].reshape(-1, local_heads, HEAD_DIM)
        scores = (
            jnp.einsum("qhd,khd->hqk", query_heads, key_heads, preferred_element_type=jnp.float32)
            * scale_factor
        )
        allowed = query_segment[:, None] == key_segment[None, :]
        return (jnp.where(allowed[None], scores, masked_score), value_heads)

    def absorb(state, block, key_segment):
        row_top, totals, summed = state
        scores, value_heads = block_scores(block, key_segment)
        new_top = jnp.maximum(row_top, jnp.max(scores, axis=-1, keepdims=True))
        factor = jnp.exp(row_top - new_top)
        weights = jnp.exp(scores - new_top)
        totals = totals * factor + jnp.sum(weights, axis=-1, keepdims=True)
        summed = summed * factor + jnp.einsum(
            "hqk,khd->hqd",
            weights.astype(jnp.bfloat16),
            value_heads,
            preferred_element_type=jnp.float32,
        )
        return (new_top, totals, summed)

    def absorb_remote(state, block, key_start):
        key_segment = segment_window(key_start, tok_dev)
        return absorb(state, block, key_segment)

    start_state = (
        jnp.full((local_heads, tok_dev, 1), masked_score, jnp.float32),
        jnp.zeros((local_heads, tok_dev, 1), jnp.float32),
        jnp.zeros((local_heads, tok_dev, HEAD_DIM), jnp.float32),
    )
    sign = 1 - 2 * (seq_index % 2)

    def swap(value):
        return lax.ppermute(value, "seq", [(i, i ^ 1) for i in range(seq_count)])

    def absorb_at(state, block, offset):
        return absorb_remote(state, block, row_start + offset * tok_dev)

    below_2 = from_behind(key_value, "seq", 2)
    above_2 = from_behind(key_value, "seq", -2)
    below_4 = from_behind(key_value, "seq", 4)
    above_4 = from_behind(key_value, "seq", -4)
    partner_own = swap(key_value)
    state = absorb(start_state, key_value, query_segment)
    partner_below_2 = swap(below_2)
    partner_above_2 = swap(above_2)
    partner_far = swap(jnp.where(sign > 0, above_4, below_4))
    state = absorb_at(state, partner_own, sign)
    state = absorb_at(state, below_2, -2)
    state = absorb_at(state, above_2, 2)
    state = absorb_at(state, partner_below_2, sign - 2)
    state = absorb_at(state, partner_above_2, sign + 2)
    state = absorb_at(state, below_4, -4)
    state = absorb_at(state, above_4, 4)
    state = absorb_at(state, partner_far, -3 * sign)
    row_top, totals, summed = state
    tp_index = lax.axis_index("tp")
    quarter = tok_dev // 4
    by_token = (summed / totals).reshape(local_heads, quarter, 4, HEAD_DIM)
    attended = jnp.transpose(by_token, (2, 1, 0, 3)).reshape(4, quarter, local_width).astype(jnp.bfloat16)
    head_term = jnp.einsum(
        "tgc,cd->tgd", attended, w_out, preferred_element_type=jnp.float32
    ).astype(jnp.bfloat16)
    head_terms = lax.all_to_all(head_term, "tp", split_axis=0, concat_axis=0, tiled=True)
    head_total = jnp.sum(head_terms.astype(jnp.float32), axis=0)
    own_tokens = lax.dynamic_index_in_dim(
        tokens.reshape(quarter, 4, model_width), tp_index, 1, keepdims=False
    )
    own_rows = own_tokens.astype(jnp.float32) + head_total + b_out
    merged_rows = layer_norm(own_rows, merge_gain, merge_bias).astype(jnp.bfloat16)
    owner_rows = owners[:, 0]
    capacity = max(2, 2 * quarter // seq_count)
    owner_table = (owner_rows[:, None] == jnp.arange(seq_count, dtype=jnp.int32)[None, :]).astype(
        jnp.int32
    )
    earlier = jnp.cumsum(owner_table, axis=0) - owner_table
    row_slot = jnp.sum(earlier * owner_table, axis=1)
    target_row = owner_rows * capacity + row_slot
    placing = (
        jnp.arange(seq_count * capacity, dtype=jnp.int32)[:, None] == target_row[None, :]
    ).astype(jnp.bfloat16)
    outgoing = jnp.dot(placing, merged_rows, preferred_element_type=jnp.float32).astype(
        jnp.bfloat16
    )
    return lax.all_to_all(outgoing, "seq", split_axis=0, concat_axis=0, tiled=True)


def solution(mesh):
    placed = (
        P("seq", None),
        P(),
        P(),
        P(None, None, "tp"),
        P(None, "tp"),
        P("tp", None),
        P(),
        P(),
        P(),
        P(),
        P("seq", None),
    )
    return jax.shard_map(
        per_device, mesh=mesh, in_specs=placed, out_specs=P("seq", "tp"), check_vma=False
    )
```
